256 devices in a mesh: req: 32 (over z, x), head: 4 (over y), blk: 2 (over core).
Axes of the slice: x: 4, y: 4, z: 8, core: 2. Of those that a mesh axis runs over, the one named last changes fastest.
Arguments:
- x_tokens: bfloat16 [32, 512, 1024], P('req', ('head', 'blk')), may hold values from -40 to 40
- query: bfloat16 [32, 512, 1024], P('req', None, ('head', 'blk')), may hold values from -200 to 200
- key_new: bfloat16 [32, 512, 1024], P('req', None, ('head', 'blk')), may hold values from -4 to 4
- value_new: bfloat16 [32, 512, 1024], P('req', None, ('head', 'blk')), may hold values from -4 to 4
- cache_keys: bfloat16 [32, 2048, 1024], P('req', None, ('head', 'blk')), may hold values from -4 to 4
- cache_values: bfloat16 [32, 2048, 1024], P('req', None, ('head', 'blk')), may hold values from -4 to 4
- prefix_keys: bfloat16 [4, 512, 1024], P(None, None, ('head', 'blk')), may hold values from -4 to 4
- prefix_values: bfloat16 [4, 512, 1024], P(None, None, ('head', 'blk')), may hold values from -4 to 4
- history_len: int32 [32], P('req'), may hold values from 512 to 2048, as said below
- group_ids: int32 [32], P('req'), may hold values from 0 to 3
- out_weight: bfloat16 [1024, 1024], P(('head', 'blk')), may hold values from -0.1875 to 0.1875
- norm_gain: float32 [1024], replicated, may hold values from 0.5 to 1.5
- router_weight: bfloat16 [1024, 16], replicated, may hold values from -0.1875 to 0.1875
- expert_gate: bfloat16 [1024, 45056], P(None, ('req', 'head')), may hold values from -0.1875 to 0.1875
- expert_up: bfloat16 [1024, 45056], P(None, ('req', 'head')), may hold values from -0.1875 to 0.1875
- expert_down: bfloat16 [45056, 1024], P(('req', 'head')), may hold values from -0.109375 to 0.109375
- expert_ids: int32 [32, 512, 2], P('req', ('head', 'blk')), may hold values from 0 to 15, all different within a row; in each aligned block of 64 rows (0 to 63, 64 to 127, ..., all dimensions but the last counted through in order) at most 16 rows name the same one
- keep_mask: int32 [32, 512, 2], P('req', ('head', 'blk')), may hold values 0 or 1
Outputs:
- y_out: bfloat16 [32, 512, 1024], P('req', ('head', 'blk'))
- new_keys: bfloat16 [32, 2560, 1024], P('req', ('head', 'blk'))
- new_values: bfloat16 [32, 2560, 1024], P('req', ('head', 'blk'))
The draws below stay inside these ranges and needn't reach their ends.
Inputs may be any that keep to these rules, and one draw needn't show every extreme that they name: `history_len`: one request has exactly 2048 used slots. `expert_ids`: the two experts of a token differ; within each aligned block of 64 tokens (one request, positions b * 64 onward) no expert is named by more than 16 choices, dropped ones included.
All inputs are finite; a program needn't handle non-finite values. No bound on the sum of `keep_mask` on one device may be relied on, other than what follows from the above.
Results may differ from the reference program's by a relative error of at most 0.0036.
Values may be sent and summed in bfloat16 or wider, within the bound.
No kernel may reach another device: no remote copies, remote signals or barrier semaphores. Data moves between devices by JAX's collectives and lax.ppermute only.
A program may use at most 64 MiB of HBM per device.

```python
import math
import jax
import jax.numpy as jnp
import numpy as np
from jax import lax

HEADS = 16
HD = 64
D = 1024
FF = 2816
EXPERTS = 16
REQUESTS = 32
STRETCH = 512
HIST = 2048
PREFIX = 512
GROUPS = 4
SLOT = 16
ROWS_BLK = 64
SHARDS = 8


def stretch_pair(key):
    base = jax.random.fold_in(key, 11)
    first, second = jax.random.split(base, 2)
    shape = (REQUESTS, STRETCH, HEADS, HD)
    keys_drawn = jnp.clip(jax.random.normal(first, shape, jnp.float32), -4.0, 4.0)
    queries = jnp.clip(2.5 * jax.random.normal(second, shape, jnp.float32), -10.0, 10.0)
    return (queries.reshape(REQUESTS, STRETCH, HEADS * HD), keys_drawn.reshape(REQUESTS, STRETCH, HEADS * HD))


def draw_query(key, part):
    return stretch_pair(key)[0].astype(jnp.bfloat16)


def draw_key_new(key, part):
    return stretch_pair(key)[1].astype(jnp.bfloat16)


def draw_x_tokens(key, part):
    first, second, third = jax.random.split(jax.random.fold_in(key, 23), 3)
    shape = (REQUESTS, STRETCH, HEADS * HD)
    row_scale = jnp.exp(jax.random.uniform(first, (REQUESTS, STRETCH, 1), jnp.float32, math.log(0.3), math.log(3.0)))
    column_scale = jnp.exp(jax.random.uniform(second, (HEADS * HD,), jnp.float32, math.log(0.3), math.log(3.0)))
    base = jnp.clip(jax.random.normal(third, shape, jnp.float32), -4.0, 4.0)
    return (base * row_scale * column_scale).astype(jnp.bfloat16)


def draw_history_len(key, part):
    first, second = jax.random.split(jax.random.fold_in(key, 37))
    lengths = jax.random.randint(first, (REQUESTS,), HIST // 4, HIST + 1)
    longest = jax.random.randint(second, (), 0, REQUESTS)
    return jnp.where(jnp.arange(REQUESTS) == longest, HIST, lengths).astype(jnp.int32)


def place_ends(values, key, low, largest):
    longest = values.shape.index(max(values.shape))
    spots = []
    for shift in (0, 1):
        where = [jax.random.randint(jax.random.fold_in(key, axis), (), 0, length) for axis, length in enumerate(values.shape)]
        where[longest] = (where[longest] + shift) % values.shape[longest]
        spots.append(tuple(where))
    return values.at[spots[0]].set(low).at[spots[1]].set(largest)


def levels(stream_key, dims, cuts, least, high):
    level = 1.0
    for dim, parts in cuts:
        draws = jax.random.uniform(jax.random.fold_in(jax.random.fold_in(stream_key, 6), dim), (parts,), jnp.float32, least / len(cuts), high / len(cuts))
        level = level * jnp.repeat(jnp.exp(draws), dims[dim] // parts).reshape((-1,) + (1,) * (len(dims) - 1 - dim))
    return level


def deal_out(rng, own, number, rows, count, top, limit, skew):
    sequence = jax.random.permutation(rng, count)
    packed, usual = shares(count, rows * top, limit, skew, True), shares(count, rows * top, limit, skew, False)
    places = jnp.arange(count)

    def named(sizes, offset_by):
        used = int((sizes > 0).sum())
        fixed = max(1, used // 4)
        passed = fixed + (places - fixed + offset_by * (used - fixed)) % max(1, count - fixed)
        return jnp.zeros((count,), jnp.int32).at[sequence[jnp.where(places < fixed, places, passed)]].set(jnp.asarray(sizes, jnp.int32))

    sizes = jnp.where(number % 4 == 0, named(packed, number // 4), named(usual, number - number // 4 - 1))
    mixed = jax.random.permutation(jax.random.fold_in(own, 3), count)
    giver, receiver = mixed[0:count // 2 * 2:2], mixed[1:count // 2 * 2:2]
    room = jnp.minimum(sizes[giver] - 1, limit - sizes[receiver]) // 2
    room = jnp.where((giver == sequence[0]) | (receiver == sequence[0]) | (sizes[receiver] == 0), 0, jnp.maximum(room, 0))
    passed = jax.random.randint(jax.random.fold_in(own, 4), (count // 2,), 0, 1 << 20) % (room + 1)
    sizes = sizes.at[giver].add(-passed).at[receiver].add(passed)
    members = jnp.searchsorted(jnp.cumsum(sizes), jnp.arange(rows * top), side="right").astype(jnp.int32)
    listing = members.reshape(top, rows).T
    listing = listing[jax.random.permutation(jax.random.fold_in(own, 1), rows)]
    offset_by = jax.random.randint(jax.random.fold_in(own, 2), (rows, 1), 0, top)
    return jnp.take_along_axis(listing, (jnp.arange(top)[None, :] + offset_by) % top, axis=1)


def shares(number_of, total, bound, slope, full):
    loads = [(1 << 20) // math.isqrt(standing ** slope) + 1 for standing in range(1, number_of + 1)]
    largest = bound if full else min(bound, max(-(-total // number_of), total * loads[0] // sum(loads)))
    least = 1 if total - largest >= number_of - 1 else 0
    holding, rest = [largest] + [least] * (number_of - 1), total - largest - least * (number_of - 1)
    while rest > 0:
        free = [i for i in range(1, number_of) if holding[i] < largest] or [i for i in range(1, number_of) if holding[i] < bound]
        mass, remaining = sum([loads[i] for i in free]), rest
        for i in free:
            extra = min(bound - holding[i], max(1, remaining * loads[i] // mass), rest)
            holding[i] = holding[i] + extra
            rest = rest - extra
    return np.array(holding)


def bell_draw(stream_key, dims, scale, bound, cuts=(), dtype=jnp.bfloat16):
    factor_of = levels(stream_key, dims, cuts, -0.22, 0.18) if cuts else 1.0
    drawn = jax.random.normal(stream_key, dims, jnp.float32) * scale * factor_of
    return jnp.minimum(jnp.maximum(drawn, -bound), bound).astype(dtype)


def setup_inputs(seed: int = 0) -> dict:
    streams_of = jax.random.split(jax.random.key(seed), 19)
    x_tokens = draw_x_tokens(jax.random.fold_in(streams_of[18], 71), 0)
    query = draw_query(jax.random.fold_in(streams_of[18], 71), 0)
    key_new = draw_key_new(jax.random.fold_in(streams_of[18], 71), 0)
    value_new = bell_draw(streams_of[3], (REQUESTS, STRETCH, D), 1.0, 4.0, ((0, 32), (2, 8)))
    cache_keys = bell_draw(streams_of[4], (REQUESTS, HIST, D), 1.0, 4.0, ((0, 32), (2, 8)))
    cache_values = bell_draw(streams_of[5], (REQUESTS, HIST, D), 1.0, 4.0, ((0, 32), (2, 8)))
    prefix_keys = bell_draw(streams_of[6], (GROUPS, PREFIX, D), 1.0, 4.0, ((2, 8),))
    prefix_values = bell_draw(streams_of[7], (GROUPS, PREFIX, D), 1.0, 4.0, ((2, 8),))
    history_len = draw_history_len(jax.random.fold_in(streams_of[18], 71), 0)
    group_ids = place_ends(jax.random.randint(streams_of[9], (REQUESTS,), 0, GROUPS), jax.random.fold_in(streams_of[9], 1), 0, GROUPS - 1).astype(jnp.int32)
    out_weight = bell_draw(streams_of[10], (D, D), D ** -0.5, 0.1875, ((0, 8),))
    norm_gain = jnp.clip(1.0 + 0.1 * jax.random.normal(streams_of[11], (D,), jnp.float32), 0.5, 1.5)
    router_weight = bell_draw(streams_of[12], (D, EXPERTS), D ** -0.5, 0.1875)
    expert_gate = bell_draw(streams_of[13], (D, EXPERTS * FF), D ** -0.5, 0.1875, ((1, 128),))
    expert_up = bell_draw(streams_of[14], (D, EXPERTS * FF), D ** -0.5, 0.1875, ((1, 128),))
    expert_down = bell_draw(streams_of[15], (EXPERTS * FF, D), FF ** -0.5, 0.109375, ((0, 128),))
    expert_ids_keys = jax.random.split(jax.random.fold_in(streams_of[16], 1), REQUESTS * STRETCH // ROWS_BLK)
    expert_ids_turns = jax.random.permutation(jax.random.fold_in(streams_of[16], 3), REQUESTS * STRETCH // ROWS_BLK)
    expert_ids = jax.vmap(lambda own, number: deal_out(jax.random.fold_in(streams_of[16], 2), own, number, ROWS_BLK, EXPERTS, 2, SLOT, 1))(expert_ids_keys, expert_ids_turns).reshape((REQUESTS, STRETCH, 2))
    keep_mask = place_ends((jax.random.randint(streams_of[17], (REQUESTS, STRETCH, 2), 0, 8) < 7).astype(jnp.int32), jax.random.fold_in(streams_of[17], 1), 0, 1)
    return {"x_tokens": x_tokens, "query": query, "key_new": key_new, "value_new": value_new, "cache_keys": cache_keys, "cache_values": cache_values, "prefix_keys": prefix_keys, "prefix_values": prefix_values, "history_len": history_len, "group_ids": group_ids, "out_weight": out_weight, "norm_gain": norm_gain, "router_weight": router_weight, "expert_gate": expert_gate, "expert_up": expert_up, "expert_down": expert_down, "expert_ids": expert_ids, "keep_mask": keep_mask}


EPSILON = 1e-06

def attend_request(operands):
    queries, keys_stretch, values_stretch, keys_cache, values_cache, keys_prefix, values_prefix, length = operands
    keys_all = jnp.concatenate([keys_prefix, keys_cache, keys_stretch], 0).reshape(-1, HEADS, HD).astype(jnp.float32)
    values_all = jnp.concatenate([values_prefix, values_cache, values_stretch], 0).reshape(-1, HEADS, HD).astype(jnp.float32)
    key_pos = jnp.arange(PREFIX + HIST + STRETCH)
    query_pos = jnp.arange(STRETCH)
    in_prefix = key_pos < PREFIX
    in_history = (key_pos >= PREFIX) & (key_pos < PREFIX + HIST) & (key_pos - PREFIX < length)
    in_stretch = (key_pos[None, :] >= PREFIX + HIST) & (key_pos[None, :] - PREFIX - HIST <= query_pos[:, None])
    visible = (in_prefix | in_history)[None, :] | in_stretch
    scores = jnp.einsum('qhd,khd->hqk', queries.reshape(STRETCH, HEADS, HD).astype(jnp.float32), keys_all) * HD ** (-0.5)
    highest = lax.optimization_barrier(jnp.max(jnp.where(visible[None], scores, -jnp.inf), axis=-1, keepdims=True))
    weights = jnp.where(visible[None], jnp.exp(scores - highest), 0.0)
    total = lax.optimization_barrier(jnp.sum(weights, axis=-1, keepdims=True))
    rounded = lax.optimization_barrier(weights.astype(jnp.bfloat16)).astype(jnp.float32)
    mixed = jnp.einsum('hqk,khd->qhd', rounded, values_all) / jnp.transpose(total, (1, 0, 2))
    return mixed.reshape(STRETCH, D).astype(jnp.bfloat16)

def extend(cache, stretch, length):
    span = jnp.arange(HIST)
    kept = jnp.where((span < length)[:, None], cache, jnp.zeros_like(cache))
    grown = jnp.concatenate([kept, jnp.zeros_like(stretch)], 0)
    return lax.dynamic_update_slice(grown, stretch, (length.astype(jnp.int32), jnp.int32(0)))

def reference(x_tokens, query, key_new, value_new, cache_keys, cache_values, prefix_keys, prefix_values, history_len, group_ids, out_weight, norm_gain, router_weight, expert_gate, expert_up, expert_down, expert_ids, keep_mask):
    chosen_keys = jnp.take(prefix_keys, group_ids, axis=0)
    chosen_values = jnp.take(prefix_values, group_ids, axis=0)
    attended = lax.map(attend_request, (query, key_new, value_new, cache_keys, cache_values, chosen_keys, chosen_values, history_len))
    tokens = REQUESTS * STRETCH
    resid = x_tokens.reshape(tokens, D).astype(jnp.float32) + jnp.dot(attended.reshape(tokens, D), out_weight, preferred_element_type=jnp.float32)
    mean_square = lax.optimization_barrier(jnp.mean(resid * resid, axis=-1, keepdims=True))
    normed = (resid * lax.rsqrt(mean_square + EPSILON) * norm_gain).astype(jnp.bfloat16)
    logits = jnp.dot(normed, router_weight, preferred_element_type=jnp.float32)
    picks = expert_ids.reshape(tokens, 2)
    chosen = jnp.take_along_axis(logits, picks, axis=1)
    keep = keep_mask.reshape(tokens, 2)
    gate_weights = jax.nn.sigmoid(chosen - chosen[:, ::-1]) * keep.astype(jnp.float32)
    blocks = tokens // ROWS_BLK
    block_picks = picks.reshape(blocks, ROWS_BLK * 2)
    onehot = (block_picks[:, :, None] == jnp.arange(EXPERTS)[None, None, :]).astype(jnp.int32)
    ranks = lax.optimization_barrier(jnp.sum((jnp.cumsum(onehot, axis=1) - 1) * onehot, axis=-1))
    places = (block_picks * (blocks * SLOT) + jnp.arange(blocks)[:, None] * SLOT + ranks).reshape(-1).astype(jnp.int32)
    sent_rows = (normed[:, None, :] * keep[:, :, None].astype(jnp.bfloat16)).reshape(-1, D)
    buffer = jnp.zeros((EXPERTS * blocks * SLOT, D), jnp.bfloat16).at[places].set(sent_rows).reshape(EXPERTS, blocks * SLOT, D)
    gate_cols = jnp.transpose(expert_gate.reshape(D, EXPERTS, FF), (1, 0, 2))
    up_cols = jnp.transpose(expert_up.reshape(D, EXPERTS, FF), (1, 0, 2))
    down_rows = expert_down.reshape(EXPERTS, FF, D)

    def serve(operands):
        slab, w_gate, w_up, w_down = operands
        gate_val = jnp.dot(slab, w_gate, preferred_element_type=jnp.float32)
        up_val = jnp.dot(slab, w_up, preferred_element_type=jnp.float32)
        hidden = (jax.nn.gelu(gate_val, approximate=True) * up_val).astype(jnp.bfloat16)
        pieces = lax.optimization_barrier(hidden).reshape(-1, SHARDS, FF // SHARDS).astype(jnp.float32)
        partial_out = jnp.einsum('nsf,sfd->snd', pieces, w_down.reshape(SHARDS, FF // SHARDS, D).astype(jnp.float32))
        return lax.optimization_barrier(jnp.sum(lax.optimization_barrier(partial_out.astype(jnp.bfloat16)).astype(jnp.float32), axis=0))
    served = lax.map(serve, (buffer, gate_cols, up_cols, down_rows)).reshape(-1, D)
    picked = jnp.take(served, places, axis=0).reshape(tokens, 2, D)
    mixture = lax.optimization_barrier(jnp.sum(picked * gate_weights[:, :, None], axis=1))
    y_out = (resid + mixture).astype(jnp.bfloat16).reshape(REQUESTS, STRETCH, D)
    new_keys = jax.vmap(extend)(cache_keys, key_new, history_len)
    new_values = jax.vmap(extend)(cache_values, value_new, history_len)
    return (y_out, new_keys, new_values)
```

```python
import jax
import jax.numpy as jnp
from jax import lax
from jax.sharding import PartitionSpec as P

HD = 64
SLOT = 16


EPSILON = 1e-06


def attend_request(operands):
    (
        queries,
        keys_stretch,
        values_stretch,
        keys_cache,
        values_cache,
        keys_prefix,
        values_prefix,
        length,
    ) = operands
    heads_here = queries.shape[1] // HD
    prefix_rows = keys_prefix.shape[0]
    history_rows = keys_cache.shape[0]
    stretch_rows = queries.shape[0]
    keys_all = jnp.concatenate([keys_prefix, keys_cache, keys_stretch], 0).reshape(
        -1, heads_here, HD
    )
    values_all = jnp.concatenate([values_prefix, values_cache, values_stretch], 0).reshape(
        -1, heads_here, HD
    )
    key_pos = jnp.arange(keys_all.shape[0])
    query_pos = jnp.arange(stretch_rows)
    in_prefix = key_pos < prefix_rows
    in_history = (
        (key_pos >= prefix_rows)
        & (key_pos < prefix_rows + history_rows)
        & (key_pos - prefix_rows < length)
    )
    in_stretch = (key_pos[None, :] >= prefix_rows + history_rows) & (
        key_pos[None, :] - prefix_rows - history_rows <= query_pos[:, None]
    )
    visible = (in_prefix | in_history)[None, :] | in_stretch
    scores = jnp.einsum(
        "qhd,khd->hqk",
        queries.reshape(stretch_rows, heads_here, HD),
        keys_all,
        preferred_element_type=jnp.float32,
    ) * HD ** (-0.5)
    highest = jnp.max(jnp.where(visible[None], scores, -jnp.inf), axis=-1, keepdims=True)
    weights = jnp.where(visible[None], jnp.exp(scores - highest), 0.0)
    total = jnp.sum(weights, axis=-1, keepdims=True)
    rounded = weights.astype(jnp.bfloat16)
    mixed = jnp.einsum(
        "hqk,khd->qhd", rounded, values_all, preferred_element_type=jnp.float32
    ) / jnp.transpose(total, (1, 0, 2))
    return mixed.reshape(stretch_rows, -1).astype(jnp.bfloat16)


def extend(cache, stretch, length):
    hist = cache.shape[0]
    rows = stretch.shape[0]
    width = cache.shape[1]
    span = jnp.arange(hist + rows)
    padded_cache = jnp.concatenate([cache, jnp.zeros((rows, width), cache.dtype)], 0)
    framed = jnp.concatenate(
        [jnp.zeros((hist, width), stretch.dtype), stretch, jnp.zeros((hist, width), stretch.dtype)], 0
    )
    shifted = lax.dynamic_slice(framed, (hist - length, jnp.int32(0)), (hist + rows, width))
    return jnp.where((span < length)[:, None], padded_cache, shifted)


def body(
    x_tokens,
    query,
    key_new,
    value_new,
    cache_keys,
    cache_values,
    prefix_keys,
    prefix_values,
    history_len,
    group_ids,
    out_weight,
    norm_gain,
    router_weight,
    expert_gate,
    expert_up,
    expert_down,
    expert_ids,
    keep_mask,
):
    grown_keys = jax.vmap(extend)(cache_keys, key_new, history_len)
    grown_values = jax.vmap(extend)(cache_values, value_new, history_len)
    new_keys, new_values = (
        lax.all_to_all(grown_keys, ("head", "blk"), split_axis=1, concat_axis=2, tiled=True),
        lax.all_to_all(grown_values, ("head", "blk"), split_axis=1, concat_axis=2, tiled=True),
    )
    chosen_keys = jnp.take(prefix_keys, group_ids, axis=0)
    chosen_values = jnp.take(prefix_values, group_ids, axis=0)
    attended = lax.map(
        attend_request,
        (
            query,
            key_new,
            value_new,
            cache_keys,
            cache_values,
            chosen_keys,
            chosen_values,
            history_len,
        ),
    )
    requests_here = x_tokens.shape[0]
    rows_here = x_tokens.shape[1]
    width = x_tokens.shape[2]
    full_weight = lax.all_gather(out_weight, ("head", "blk"), axis=0, tiled=True)
    by_token = lax.all_to_all(attended, ("head", "blk"), split_axis=1, concat_axis=2, tiled=True)
    projected = jnp.einsum(
        "rqf,fd->rqd", by_token, full_weight, preferred_element_type=jnp.float32
    )
    resid = x_tokens.astype(jnp.float32) + projected
    mean_square = jnp.mean(resid * resid, axis=-1, keepdims=True)
    normed = (resid * lax.rsqrt(mean_square + EPSILON) * norm_gain).astype(jnp.bfloat16)
    logits = jnp.dot(normed.reshape(-1, width), router_weight, preferred_element_type=jnp.float32)
    picks = expert_ids.reshape(-1, 2)
    chosen = jnp.take_along_axis(logits, picks, axis=1)
    keep = keep_mask.reshape(-1, 2)
    gate_weights = jax.nn.sigmoid(chosen - chosen[:, ::-1]) * keep.astype(jnp.float32)
    experts = router_weight.shape[1]
    slots_here = requests_here * SLOT
    block_picks = expert_ids.reshape(requests_here, rows_here * 2)
    onehot = (block_picks[:, :, None] == jnp.arange(experts)[None, None, :]).astype(jnp.int32)
    ranks = jnp.sum((jnp.cumsum(onehot, axis=1) - 1) * onehot, axis=-1)
    places = (block_picks * slots_here + jnp.arange(requests_here)[:, None] * SLOT + ranks).reshape(
        -1
    )
    sent_rows = (normed[:, :, None, :] * keep_mask[:, :, :, None].astype(jnp.bfloat16)).reshape(
        -1, width
    )
    buffer = jnp.zeros((experts * slots_here, width), jnp.bfloat16).at[places].set(sent_rows)
    holders = lax.axis_size("req") // experts
    outgoing = jnp.repeat(buffer.reshape(experts, slots_here, width), holders, axis=0)
    arrived = lax.all_to_all(outgoing, "req", split_axis=0, concat_axis=0, tiled=True)
    gathered = lax.all_gather(arrived, "head", axis=0, tiled=False)
    flat_rows = gathered.reshape(-1, width)
    gate_val = jnp.dot(flat_rows, expert_gate, preferred_element_type=jnp.float32)
    up_val = jnp.dot(flat_rows, expert_up, preferred_element_type=jnp.float32)
    hidden = (jax.nn.gelu(gate_val, approximate=True) * up_val).astype(jnp.bfloat16)
    partial = (
        jnp.dot(hidden, expert_down, preferred_element_type=jnp.float32)
        .astype(jnp.bfloat16)
        .reshape(gathered.shape)
    )
    shard_parts = lax.all_to_all(partial, "head", split_axis=0, concat_axis=0, tiled=True)
    half_sum = jnp.sum(shard_parts.astype(jnp.float32), axis=0).astype(jnp.bfloat16)
    returned = lax.all_to_all(half_sum, "req", split_axis=0, concat_axis=0, tiled=True)
    combined = jnp.sum(
        returned.reshape(experts, holders, slots_here, width), axis=1, dtype=jnp.float32
    ).reshape(experts * slots_here, width)
    picked = jnp.take(combined, places, axis=0).reshape(-1, 2, width)
    mixture = jnp.sum(picked * gate_weights[:, :, None], axis=1)
    y_out = (
        (resid.reshape(-1, width) + mixture)
        .astype(jnp.bfloat16)
        .reshape(requests_here, rows_here, width)
    )
    return (y_out, new_keys, new_values)


def solution(mesh):
    return jax.shard_map(
        body,
        mesh=mesh,
        in_specs=(
            P("req", ("head", "blk"), None),
            P("req", None, ("head", "blk")),
            P("req", None, ("head", "blk")),
            P("req", None, ("head", "blk")),
            P("req", None, ("head", "blk")),
            P("req", None, ("head", "blk")),
            P(None, None, ("head", "blk")),
            P(None, None, ("head", "blk")),
            P("req"),
            P("req"),
            P(("head", "blk"), None),
            P(),
            P(),
            P(None, ("req", "head")),
            P(None, ("req", "head")),
            P(("req", "head"), None),
            P("req", ("head", "blk"), None),
            P("req", ("head", "blk"), None),
        ),
        out_specs=(
            P("req", ("head", "blk"), None),
            P("req", ("head", "blk"), None),
            P("req", ("head", "blk"), None),
        ),
        check_vma=False,
    )
```

```python
import jax
import jax.numpy as jnp
from jax import lax
from jax.sharding import PartitionSpec as P

HD = 64
SLOT = 16


EPSILON = 1e-06


def attend_request(operands):
    (
        queries,
        keys_stretch,
        values_stretch,
        keys_cache,
        values_cache,
        keys_prefix,
        values_prefix,
        length,
    ) = operands
    heads_here = queries.shape[1] // HD
    prefix_rows = keys_prefix.shape[0]
    history_rows = keys_cache.shape[0]
    stretch_rows = queries.shape[0]
    keys_all = jnp.concatenate([keys_prefix, keys_cache, keys_stretch], 0).reshape(
        -1, heads_here, HD
    )
    values_all = jnp.concatenate([values_prefix, values_cache, values_stretch], 0).reshape(
        -1, heads_here, HD
    )
    key_pos = jnp.arange(keys_all.shape[0])
    query_pos = jnp.arange(stretch_rows)
    in_prefix = key_pos < prefix_rows
    in_history = (
        (key_pos >= prefix_rows)
        & (key_pos < prefix_rows + history_rows)
        & (key_pos - prefix_rows < length)
    )
    in_stretch = (key_pos[None, :] >= prefix_rows + history_rows) & (
        key_pos[None, :] - prefix_rows - history_rows <= query_pos[:, None]
    )
    visible = (in_prefix | in_history)[None, :] | in_stretch
    scores = jnp.einsum(
        "qhd,khd->hqk",
        queries.reshape(stretch_rows, heads_here, HD),
        keys_all,
        preferred_element_type=jnp.float32,
    ) * HD ** (-0.5)
    highest = jnp.max(jnp.where(visible[None], scores, -jnp.inf), axis=-1, keepdims=True)
    weights = jnp.where(visible[None], jnp.exp(scores - highest), 0.0)
    total = jnp.sum(weights, axis=-1, keepdims=True)
    rounded = weights.astype(jnp.bfloat16)
    mixed = jnp.einsum(
        "hqk,khd->qhd", rounded, values_all, preferred_element_type=jnp.float32
    ) / jnp.transpose(total, (1, 0, 2))
    return mixed.reshape(stretch_rows, -1).astype(jnp.bfloat16)


def extend(cache, stretch, length):
    hist = cache.shape[0]
    rows = stretch.shape[0]
    width = cache.shape[1]
    span = jnp.arange(hist + rows)
    padded_cache = jnp.concatenate([cache, jnp.zeros((rows, width), cache.dtype)], 0)
    framed = jnp.concatenate(
        [jnp.zeros((hist, width), stretch.dtype), stretch, jnp.zeros((hist, width), stretch.dtype)], 0
    )
    shifted = lax.dynamic_slice(framed, (hist - length, jnp.int32(0)), (hist + rows, width))
    return jnp.where((span < length)[:, None], padded_cache, shifted)


def to_positions(grown):
    groups = lax.axis_size(("head", "blk"))
    lead, rows, width = grown.shape
    parts = grown.reshape(lead, groups, rows // groups, width)
    got = lax.all_to_all(parts, ("head", "blk"), split_axis=1, concat_axis=1, tiled=True)
    return jnp.transpose(got, (0, 2, 1, 3)).reshape(lead, rows // groups, groups * width)


def body(
    x_tokens,
    query,
    key_new,
    value_new,
    cache_keys,
    cache_values,
    prefix_keys,
    prefix_values,
    history_len,
    group_ids,
    out_weight,
    norm_gain,
    router_weight,
    expert_gate,
    expert_up,
    expert_down,
    expert_ids,
    keep_mask,
):
    grown_keys = jax.vmap(extend)(cache_keys, key_new, history_len)
    grown_values = jax.vmap(extend)(cache_values, value_new, history_len)
    new_keys = to_positions(grown_keys)
    new_values = to_positions(grown_values)
    chosen_keys = jnp.take(prefix_keys, group_ids, axis=0)
    chosen_values = jnp.take(prefix_values, group_ids, axis=0)
    attended = lax.map(
        attend_request,
        (
            query,
            key_new,
            value_new,
            cache_keys,
            cache_values,
            chosen_keys,
            chosen_values,
            history_len,
        ),
    )
    requests_here = x_tokens.shape[0]
    rows_here = x_tokens.shape[1]
    width = x_tokens.shape[2]
    full_weight = lax.all_gather(out_weight, ("head", "blk"), axis=0, tiled=True)
    by_token = lax.all_to_all(attended, ("head", "blk"), split_axis=1, concat_axis=2, tiled=True)
    projected = jnp.einsum(
        "rqf,fd->rqd", by_token, full_weight, preferred_element_type=jnp.float32
    )
    resid = x_tokens.astype(jnp.float32) + projected
    mean_square = jnp.mean(resid * resid, axis=-1, keepdims=True)
    normed = (resid * lax.rsqrt(mean_square + EPSILON) * norm_gain).astype(jnp.bfloat16)
    logits = jnp.dot(normed.reshape(-1, width), router_weight, preferred_element_type=jnp.float32)
    picks = expert_ids.reshape(-1, 2)
    chosen = jnp.take_along_axis(logits, picks, axis=1)
    keep = keep_mask.reshape(-1, 2)
    gate_weights = jax.nn.sigmoid(chosen - chosen[:, ::-1]) * keep.astype(jnp.float32)
    experts = router_weight.shape[1]
    slots_here = requests_here * SLOT
    block_picks = expert_ids.reshape(requests_here, rows_here * 2)
    onehot = (block_picks[:, :, None] == jnp.arange(experts)[None, None, :]).astype(jnp.int32)
    ranks = jnp.sum((jnp.cumsum(onehot, axis=1) - 1) * onehot, axis=-1)
    places = (block_picks * slots_here + jnp.arange(requests_here)[:, None] * SLOT + ranks).reshape(
        -1
    )
    sent_rows = (normed[:, :, None, :] * keep_mask[:, :, :, None].astype(jnp.bfloat16)).reshape(
        -1, width
    )
    buffer = jnp.zeros((experts * slots_here, width), jnp.bfloat16).at[places].set(sent_rows)
    holders = lax.axis_size("req") // experts
    outgoing = jnp.repeat(buffer.reshape(experts, slots_here, width), holders, axis=0)
    arrived = lax.all_to_all(outgoing, "req", split_axis=0, concat_axis=0, tiled=True)
    gathered = lax.all_gather(arrived, "head", axis=0, tiled=False)
    flat_rows = gathered.reshape(-1, width)
    gate_val = jnp.dot(flat_rows, expert_gate, preferred_element_type=jnp.float32)
    up_val = jnp.dot(flat_rows, expert_up, preferred_element_type=jnp.float32)
    hidden = (jax.nn.gelu(gate_val, approximate=True) * up_val).astype(jnp.bfloat16)
    partial = (
        jnp.dot(hidden, expert_down, preferred_element_type=jnp.float32)
        .astype(jnp.bfloat16)
        .reshape(gathered.shape)
    )
    shard_parts = lax.all_to_all(partial, "head", split_axis=0, concat_axis=0, tiled=True)
    half_sum = jnp.sum(shard_parts.astype(jnp.float32), axis=0).astype(jnp.bfloat16)
    returned = lax.all_to_all(half_sum, "req", split_axis=0, concat_axis=0, tiled=True)
    combined = jnp.sum(
        returned.reshape(experts, holders, slots_here, width), axis=1, dtype=jnp.float32
    ).reshape(experts * slots_here, width)
    picked = jnp.take(combined, places, axis=0).reshape(-1, 2, width)
    mixture = jnp.sum(picked * gate_weights[:, :, None], axis=1)
    y_out = (
        (resid.reshape(-1, width) + mixture)
        .astype(jnp.bfloat16)
        .reshape(requests_here, rows_here, width)
    )
    return (y_out, new_keys, new_values)


def solution(mesh):
    return jax.shard_map(
        body,
        mesh=mesh,
        in_specs=(
            P("req", ("head", "blk"), None),
            P("req", None, ("head", "blk")),
            P("req", None, ("head", "blk")),
            P("req", None, ("head", "blk")),
            P("req", None, ("head", "blk")),
            P("req", None, ("head", "blk")),
            P(None, None, ("head", "blk")),
            P(None, None, ("head", "blk")),
            P("req"),
            P("req"),
            P(("head", "blk"), None),
            P(),
            P(),
            P(None, ("req", "head")),
            P(None, ("req", "head")),
            P(("req", "head"), None),
            P("req", ("head", "blk"), None),
            P("req", ("head", "blk"), None),
        ),
        out_specs=(
            P("req", ("head", "blk"), None),
            P("req", ("head", "blk"), None),
            P("req", ("head", "blk"), None),
        ),
        check_vma=False,
    )
```

```python
import jax
import jax.numpy as jnp
from jax import lax
from jax.sharding import PartitionSpec as P

HD = 64
SLOT = 16


EPSILON = 1e-06


def attend_request(operands):
    (
        queries,
        keys_stretch,
        values_stretch,
        keys_cache,
        values_cache,
        keys_prefix,
        values_prefix,
        length,
    ) = operands
    heads_here = queries.shape[1] // HD
    prefix_rows = keys_prefix.shape[0]
    history_rows = keys_cache.shape[0]
    stretch_rows = queries.shape[0]
    keys_all = jnp.concatenate([keys_prefix, keys_cache, keys_stretch], 0).reshape(
        -1, heads_here, HD
    )
    values_all = jnp.concatenate([values_prefix, values_cache, values_stretch], 0).reshape(
        -1, heads_here, HD
    )
    key_pos = jnp.arange(keys_all.shape[0])
    query_pos = jnp.arange(stretch_rows)
    in_prefix = key_pos < prefix_rows
    in_history = (
        (key_pos >= prefix_rows)
        & (key_pos < prefix_rows + history_rows)
        & (key_pos - prefix_rows < length)
    )
    in_stretch = (key_pos[None, :] >= prefix_rows + history_rows) & (
        key_pos[None, :] - prefix_rows - history_rows <= query_pos[:, None]
    )
    visible = (in_prefix | in_history)[None, :] | in_stretch
    scores = jnp.einsum(
        "qhd,khd->hqk",
        queries.reshape(stretch_rows, heads_here, HD),
        keys_all,
        preferred_element_type=jnp.float32,
    ) * HD ** (-0.5)
    highest = jnp.max(jnp.where(visible[None], scores, -jnp.inf), axis=-1, keepdims=True)
    weights = jnp.where(visible[None], jnp.exp(scores - highest), 0.0)
    total = jnp.sum(weights, axis=-1, keepdims=True)
    rounded = weights.astype(jnp.bfloat16)
    mixed = jnp.einsum(
        "hqk,khd->qhd", rounded, values_all, preferred_element_type=jnp.float32
    ) / jnp.transpose(total, (1, 0, 2))
    return mixed.reshape(stretch_rows, -1).astype(jnp.bfloat16)


def extend(cache, stretch, length):
    hist = cache.shape[0]
    rows = stretch.shape[0]
    width = cache.shape[1]
    span = jnp.arange(hist + rows)
    padded_cache = jnp.concatenate([cache, jnp.zeros((rows, width), cache.dtype)], 0)
    framed = jnp.concatenate(
        [jnp.zeros((hist, width), stretch.dtype), stretch, jnp.zeros((hist, width), stretch.dtype)], 0
    )
    shifted = lax.dynamic_slice(framed, (hist - length, jnp.int32(0)), (hist + rows, width))
    return jnp.where((span < length)[:, None], padded_cache, shifted)


def to_positions(grown):
    groups = lax.axis_size(("head", "blk"))
    lead, rows, width = grown.shape
    parts = grown.reshape(lead, groups, rows // groups, width)
    got = lax.all_to_all(parts, ("head", "blk"), split_axis=1, concat_axis=1, tiled=True)
    return jnp.transpose(got, (0, 2, 1, 3)).reshape(lead, rows // groups, groups * width)


def body(
    x_tokens,
    query,
    key_new,
    value_new,
    cache_keys,
    cache_values,
    prefix_keys,
    prefix_values,
    history_len,
    group_ids,
    out_weight,
    norm_gain,
    router_weight,
    expert_gate,
    expert_up,
    expert_down,
    expert_ids,
    keep_mask,
):
    grown_keys = jax.vmap(extend)(cache_keys, key_new, history_len)
    grown_values = jax.vmap(extend)(cache_values, value_new, history_len)
    new_keys = to_positions(grown_keys)
    new_values = to_positions(grown_values)
    chosen_keys = jnp.take(prefix_keys, group_ids, axis=0)
    chosen_values = jnp.take(prefix_values, group_ids, axis=0)
    attended = lax.map(
        attend_request,
        (
            query,
            key_new,
            value_new,
            cache_keys,
            cache_values,
            chosen_keys,
            chosen_values,
            history_len,
        ),
    )
    requests_here = x_tokens.shape[0]
    rows_here = x_tokens.shape[1]
    width = x_tokens.shape[2]
    full_weight = lax.all_gather(out_weight, ("head", "blk"), axis=0, tiled=True)
    by_token = lax.all_to_all(attended, ("head", "blk"), split_axis=1, concat_axis=2, tiled=True)
    projected = jnp.einsum(
        "rqf,fd->rqd", by_token, full_weight, preferred_element_type=jnp.float32
    )
    resid = x_tokens.astype(jnp.float32) + projected
    mean_square = jnp.mean(resid * resid, axis=-1, keepdims=True)
    normed = (resid * lax.rsqrt(mean_square + EPSILON) * norm_gain).astype(jnp.bfloat16)
    logits = jnp.dot(normed.reshape(-1, width), router_weight, preferred_element_type=jnp.float32)
    picks = expert_ids.reshape(-1, 2)
    chosen = jnp.take_along_axis(logits, picks, axis=1)
    keep = keep_mask.reshape(-1, 2)
    gate_weights = jax.nn.sigmoid(chosen - chosen[:, ::-1]) * keep.astype(jnp.float32)
    experts = router_weight.shape[1]
    slots_here = requests_here * SLOT
    block_picks = expert_ids.reshape(requests_here, rows_here * 2)
    onehot = (block_picks[:, :, None] == jnp.arange(experts)[None, None, :]).astype(jnp.int32)
    ranks = jnp.sum((jnp.cumsum(onehot, axis=1) - 1) * onehot, axis=-1)
    places = (block_picks * slots_here + jnp.arange(requests_here)[:, None] * SLOT + ranks).reshape(
        -1
    )
    sent_rows = (normed[:, :, None, :] * keep_mask[:, :, :, None].astype(jnp.bfloat16)).reshape(
        -1, width
    )
    buffer = jnp.zeros((experts * slots_here, width), jnp.bfloat16).at[places].set(sent_rows)
    holders = lax.axis_size("req") // experts
    new_keys, new_values, buffer = lax.optimization_barrier((new_keys, new_values, buffer))
    slabs = buffer.reshape(experts, slots_here, width)
    chunks = 2
    step = slots_here // chunks
    pieces = []
    for c in range(chunks):
        piece = slabs[:, c * step:(c + 1) * step]
        outgoing = jnp.repeat(piece, holders, axis=0)
        arrived = lax.all_to_all(outgoing, "req", split_axis=0, concat_axis=0, tiled=True)
        gathered = lax.all_gather(arrived, "head", axis=0, tiled=False)
        flat_rows = gathered.reshape(-1, width)
        gate_val = jnp.dot(flat_rows, expert_gate, preferred_element_type=jnp.float32)
        up_val = jnp.dot(flat_rows, expert_up, preferred_element_type=jnp.float32)
        hidden = (jax.nn.gelu(gate_val, approximate=True) * up_val).astype(jnp.bfloat16)
        partial = (
            jnp.dot(hidden, expert_down, preferred_element_type=jnp.float32)
            .astype(jnp.bfloat16)
            .reshape(gathered.shape)
        )
        shard_parts = lax.all_to_all(partial, "head", split_axis=0, concat_axis=0, tiled=True)
        half_sum = jnp.sum(shard_parts.astype(jnp.float32), axis=0).astype(jnp.bfloat16)
        returned = lax.all_to_all(half_sum, "req", split_axis=0, concat_axis=0, tiled=True)
        pieces.append(
            jnp.sum(returned.reshape(experts, holders, step, width), axis=1, dtype=jnp.float32)
        )
    combined = jnp.concatenate(pieces, axis=1).reshape(experts * slots_here, width)
    picked = jnp.take(combined, places, axis=0).reshape(-1, 2, width)
    mixture = jnp.sum(picked * gate_weights[:, :, None], axis=1)
    y_out = (
        (resid.reshape(-1, width) + mixture)
        .astype(jnp.bfloat16)
        .reshape(requests_here, rows_here, width)
    )
    return (y_out, new_keys, new_values)


def solution(mesh):
    return jax.shard_map(
        body,
        mesh=mesh,
        in_specs=(
            P("req", ("head", "blk"), None),
            P("req", None, ("head", "blk")),
            P("req", None, ("head", "blk")),
            P("req", None, ("head", "blk")),
            P("req", None, ("head", "blk")),
            P("req", None, ("head", "blk")),
            P(None, None, ("head", "blk")),
            P(None, None, ("head", "blk")),
            P("req"),
            P("req"),
            P(("head", "blk"), None),
            P(),
            P(),
            P(None, ("req", "head")),
            P(None, ("req", "head")),
            P(("req", "head"), None),
            P("req", ("head", "blk"), None),
            P("req", ("head", "blk"), None),
        ),
        out_specs=(
            P("req", ("head", "blk"), None),
            P("req", ("head", "blk"), None),
            P("req", ("head", "blk"), None),
        ),
        check_vma=False,
    )
```

```python
import jax
import jax.numpy as jnp
from jax import lax
from jax.sharding import PartitionSpec as P

HD = 64
SLOT = 16


EPSILON = 1e-06


def attend_request(operands):
    (
        queries,
        keys_stretch,
        values_stretch,
        keys_cache,
        values_cache,
        keys_prefix,
        values_prefix,
        length,
    ) = operands
    heads_here = queries.shape[1] // HD
    prefix_rows = keys_prefix.shape[0]
    history_rows = keys_cache.shape[0]
    stretch_rows = queries.shape[0]
    keys_all = jnp.concatenate([keys_prefix, keys_cache, keys_stretch], 0).reshape(
        -1, heads_here, HD
    )
    values_all = jnp.concatenate([values_prefix, values_cache, values_stretch], 0).reshape(
        -1, heads_here, HD
    )
    key_pos = jnp.arange(keys_all.shape[0])
    query_pos = jnp.arange(stretch_rows)
    in_prefix = key_pos < prefix_rows
    in_history = (
        (key_pos >= prefix_rows)
        & (key_pos < prefix_rows + history_rows)
        & (key_pos - prefix_rows < length)
    )
    in_stretch = (key_pos[None, :] >= prefix_rows + history_rows) & (
        key_pos[None, :] - prefix_rows - history_rows <= query_pos[:, None]
    )
    visible = (in_prefix | in_history)[None, :] | in_stretch
    scores = jnp.einsum(
        "qhd,khd->hqk",
        queries.reshape(stretch_rows, heads_here, HD),
        keys_all,
        preferred_element_type=jnp.float32,
    ) * HD ** (-0.5)
    highest = jnp.max(jnp.where(visible[None], scores, -jnp.inf), axis=-1, keepdims=True)
    weights = jnp.where(visible[None], jnp.exp(scores - highest), 0.0)
    total = jnp.sum(weights, axis=-1, keepdims=True)
    rounded = weights.astype(jnp.bfloat16)
    mixed = jnp.einsum(
        "hqk,khd->qhd", rounded, values_all, preferred_element_type=jnp.float32
    ) / jnp.transpose(total, (1, 0, 2))
    return mixed.reshape(stretch_rows, -1).astype(jnp.bfloat16)


def extend(cache, stretch, length):
    hist = cache.shape[0]
    rows = stretch.shape[0]
    width = cache.shape[1]
    span = jnp.arange(hist + rows)
    padded_cache = jnp.concatenate([cache, jnp.zeros((rows, width), cache.dtype)], 0)
    framed = jnp.concatenate(
        [jnp.zeros((hist, width), stretch.dtype), stretch, jnp.zeros((hist, width), stretch.dtype)], 0
    )
    shifted = lax.dynamic_slice(framed, (hist - length, jnp.int32(0)), (hist + rows, width))
    return jnp.where((span < length)[:, None], padded_cache, shifted)


def to_positions(grown):
    groups = lax.axis_size(("head", "blk"))
    lead, rows, width = grown.shape
    parts = grown.reshape(lead, groups, rows // groups, width)
    got = lax.all_to_all(parts, ("head", "blk"), split_axis=1, concat_axis=1, tiled=True)
    return jnp.transpose(got, (0, 2, 1, 3)).reshape(lead, rows // groups, groups * width)


def layer(
    x_tokens,
    query,
    key_new,
    value_new,
    cache_keys,
    cache_values,
    prefix_keys,
    prefix_values,
    history_len,
    group_ids,
    out_weight,
    norm_gain,
    router_weight,
    expert_gate,
    expert_up,
    expert_down,
    expert_ids,
    keep_mask,
):
    grown_keys = jax.vmap(extend)(cache_keys, key_new, history_len)
    grown_values = jax.vmap(extend)(cache_values, value_new, history_len)
    new_keys = to_positions(grown_keys)
    new_values = to_positions(grown_values)
    chosen_keys = jnp.take(prefix_keys, group_ids, axis=0)
    chosen_values = jnp.take(prefix_values, group_ids, axis=0)
    attended = attend_request(
        (
            query[0],
            key_new[0],
            value_new[0],
            cache_keys[0],
            cache_values[0],
            chosen_keys[0],
            chosen_values[0],
            history_len[0],
        )
    )[None]
    requests_here = x_tokens.shape[0]
    rows_here = x_tokens.shape[1]
    width = x_tokens.shape[2]
    full_weight = lax.all_gather(out_weight, ("head", "blk"), axis=0, tiled=True)
    by_token = lax.all_to_all(attended, ("head", "blk"), split_axis=1, concat_axis=2, tiled=True)
    projected = jnp.einsum(
        "rqf,fd->rqd", by_token, full_weight, preferred_element_type=jnp.float32
    )
    resid = x_tokens.astype(jnp.float32) + projected
    mean_square = jnp.mean(resid * resid, axis=-1, keepdims=True)
    normed = (resid * lax.rsqrt(mean_square + EPSILON) * norm_gain).astype(jnp.bfloat16)
    logits = jnp.dot(normed.reshape(-1, width), router_weight, preferred_element_type=jnp.float32)
    picks = expert_ids.reshape(-1, 2)
    chosen = jnp.take_along_axis(logits, picks, axis=1)
    keep = keep_mask.reshape(-1, 2)
    gate_weights = jax.nn.sigmoid(chosen - chosen[:, ::-1]) * keep.astype(jnp.float32)
    experts = router_weight.shape[1]
    slots_here = requests_here * SLOT
    block_picks = expert_ids.reshape(requests_here, rows_here * 2)
    onehot = (block_picks[:, :, None] == jnp.arange(experts)[None, None, :]).astype(jnp.int32)
    ranks = jnp.sum((jnp.cumsum(onehot, axis=1) - 1) * onehot, axis=-1)
    places = (block_picks * slots_here + jnp.arange(requests_here)[:, None] * SLOT + ranks).reshape(
        -1
    )
    sent_rows = (normed[:, :, None, :] * keep_mask[:, :, :, None].astype(jnp.bfloat16)).reshape(
        -1, width
    )
    buffer = jnp.zeros((experts * slots_here, width), jnp.bfloat16).at[places].set(sent_rows)
    holders = lax.axis_size("req") // experts
    pair = [(r, r ^ 1) for r in range(lax.axis_size("req"))]
    other_gate = lax.ppermute(expert_gate, "req", pair)
    other_up = lax.ppermute(expert_up, "req", pair)
    other_down = lax.ppermute(expert_down, "req", pair)
    both_gate = jnp.stack([expert_gate, other_gate])
    both_up = jnp.stack([expert_up, other_up])
    both_down = jnp.stack([expert_down, other_down])
    step = slots_here // holders
    outgoing = buffer.reshape(experts * holders, step, width)
    arrived = lax.all_to_all(outgoing, "req", split_axis=0, concat_axis=0, tiled=True)
    gathered = lax.all_gather(arrived, "head", axis=0, tiled=False)
    flat_rows = gathered.reshape(-1, width)
    gate_val = jnp.einsum("nd,sdf->snf", flat_rows, both_gate, preferred_element_type=jnp.float32)
    up_val = jnp.einsum("nd,sdf->snf", flat_rows, both_up, preferred_element_type=jnp.float32)
    hidden = (jax.nn.gelu(gate_val, approximate=True) * up_val).astype(jnp.bfloat16)
    blocks_out = jnp.einsum(
        "snf,sfd->snd", hidden, both_down, preferred_element_type=jnp.float32
    ).astype(jnp.bfloat16)
    pair_sum = jnp.sum(blocks_out.astype(jnp.float32), axis=0).astype(jnp.bfloat16)
    shard_parts = lax.all_to_all(
        pair_sum.reshape(gathered.shape), "head", split_axis=0, concat_axis=0, tiled=True
    )
    full_sum = jnp.sum(shard_parts.astype(jnp.float32), axis=0).astype(jnp.bfloat16)
    returned = lax.all_to_all(full_sum, "req", split_axis=0, concat_axis=0, tiled=True)
    combined = returned.astype(jnp.float32).reshape(experts * slots_here, width)
    picked = jnp.take(combined, places, axis=0).reshape(-1, 2, width)
    mixture = jnp.sum(picked * gate_weights[:, :, None], axis=1)
    y_out = (
        (resid.reshape(-1, width) + mixture)
        .astype(jnp.bfloat16)
        .reshape(requests_here, rows_here, width)
    )
    return (y_out, new_keys, new_values)


def solution(mesh):
    return jax.shard_map(
        layer,
        mesh=mesh,
        in_specs=(
            P("req", ("head", "blk"), None),
            P("req", None, ("head", "blk")),
            P("req", None, ("head", "blk")),
            P("req", None, ("head", "blk")),
            P("req", None, ("head", "blk")),
            P("req", None, ("head", "blk")),
            P(None, None, ("head", "blk")),
            P(None, None, ("head", "blk")),
            P("req"),
            P("req"),
            P(("head", "blk"), None),
            P(),
            P(),
            P(None, ("req", "head")),
            P(None, ("req", "head")),
            P(("req", "head"), None),
            P("req", ("head", "blk"), None),
            P("req", ("head", "blk"), None),
        ),
        out_specs=(
            P("req", ("head", "blk"), None),
            P("req", ("head", "blk"), None),
            P("req", ("head", "blk"), None),
        ),
        check_vma=False,
    )
```

```python
import jax
import jax.numpy as jnp
from jax import lax
from jax.sharding import PartitionSpec as P

HD = 64
SLOT = 16


EPSILON = 1e-06


def attend_request(operands):
    (
        queries,
        keys_stretch,
        values_stretch,
        keys_cache,
        values_cache,
        keys_prefix,
        values_prefix,
        length,
    ) = operands
    heads_here = queries.shape[1] // HD
    prefix_rows = keys_prefix.shape[0]
    history_rows = keys_cache.shape[0]
    stretch_rows = queries.shape[0]
    keys_all = jnp.concatenate([keys_prefix, keys_cache, keys_stretch], 0).reshape(
        -1, heads_here, HD
    )
    values_all = jnp.concatenate([values_prefix, values_cache, values_stretch], 0).reshape(
        -1, heads_here, HD
    )
    key_pos = jnp.arange(keys_all.shape[0])
    query_pos = jnp.arange(stretch_rows)
    in_prefix = key_pos < prefix_rows
    in_history = (
        (key_pos >= prefix_rows)
        & (key_pos < prefix_rows + history_rows)
        & (key_pos - prefix_rows < length)
    )
    in_stretch = (key_pos[None, :] >= prefix_rows + history_rows) & (
        key_pos[None, :] - prefix_rows - history_rows <= query_pos[:, None]
    )
    visible = (in_prefix | in_history)[None, :] | in_stretch
    scores = jnp.einsum(
        "qhd,khd->hqk",
        queries.reshape(stretch_rows, heads_here, HD),
        keys_all,
        preferred_element_type=jnp.float32,
    ) * HD ** (-0.5)
    highest = jnp.max(jnp.where(visible[None], scores, -jnp.inf), axis=-1, keepdims=True)
    weights = jnp.where(visible[None], jnp.exp(scores - highest), 0.0)
    total = jnp.sum(weights, axis=-1, keepdims=True)
    rounded = weights.astype(jnp.bfloat16)
    mixed = jnp.einsum(
        "hqk,khd->qhd", rounded, values_all, preferred_element_type=jnp.float32
    ) / jnp.transpose(total, (1, 0, 2))
    return mixed.reshape(stretch_rows, -1).astype(jnp.bfloat16)


def extend(cache, stretch, length):
    hist = cache.shape[0]
    rows = stretch.shape[0]
    width = cache.shape[1]
    span = jnp.arange(hist + rows)
    padded_cache = jnp.concatenate([cache, jnp.zeros((rows, width), cache.dtype)], 0)
    framed = jnp.concatenate(
        [jnp.zeros((hist, width), stretch.dtype), stretch, jnp.zeros((hist, width), stretch.dtype)], 0
    )
    shifted = lax.dynamic_slice(framed, (hist - length, jnp.int32(0)), (hist + rows, width))
    return jnp.where((span < length)[:, None], padded_cache, shifted)


def to_positions(grown_keys, grown_values):
    groups = lax.axis_size(("head", "blk"))
    me = lax.axis_index(("head", "blk"))
    lead, rows, width = grown_keys.shape
    span = rows // groups
    parts = jnp.stack([grown_keys[0], grown_values[0]]).reshape(2, groups, span, width)
    blocks = [lax.dynamic_index_in_dim(parts, me, axis=1, keepdims=False)]
    for k in range(1, groups):
        block = lax.dynamic_index_in_dim(parts, (me + k) % groups, axis=1, keepdims=False)
        perm = [(i, (i + k) % groups) for i in range(groups)]
        blocks.append(lax.ppermute(block, ("head", "blk"), perm))
    stacked = jnp.stack(blocks, axis=1)
    order = (me - jnp.arange(groups)) % groups
    by_source = jnp.take(stacked, order, axis=1)
    joined = jnp.transpose(by_source, (0, 2, 1, 3)).reshape(2, lead, span, groups * width)
    return joined[0], joined[1]


def layer(
    x_tokens,
    query,
    key_new,
    value_new,
    cache_keys,
    cache_values,
    prefix_keys,
    prefix_values,
    history_len,
    group_ids,
    out_weight,
    norm_gain,
    router_weight,
    expert_gate,
    expert_up,
    expert_down,
    expert_ids,
    keep_mask,
):
    grown_keys = jax.vmap(extend)(cache_keys, key_new, history_len)
    grown_values = jax.vmap(extend)(cache_values, value_new, history_len)
    new_keys, new_values = to_positions(grown_keys, grown_values)
    chosen_keys = jnp.take(prefix_keys, group_ids, axis=0)
    chosen_values = jnp.take(prefix_values, group_ids, axis=0)
    attended = attend_request(
        (
            query[0],
            key_new[0],
            value_new[0],
            cache_keys[0],
            cache_values[0],
            chosen_keys[0],
            chosen_values[0],
            history_len[0],
        )
    )[None]
    requests_here = x_tokens.shape[0]
    rows_here = x_tokens.shape[1]
    width = x_tokens.shape[2]
    full_weight = lax.all_gather(out_weight, ("head", "blk"), axis=0, tiled=True)
    by_token = lax.all_to_all(attended, ("head", "blk"), split_axis=1, concat_axis=2, tiled=True)
    projected = jnp.einsum(
        "rqf,fd->rqd", by_token, full_weight, preferred_element_type=jnp.float32
    )
    resid = x_tokens.astype(jnp.float32) + projected
    mean_square = jnp.mean(resid * resid, axis=-1, keepdims=True)
    normed = (resid * lax.rsqrt(mean_square + EPSILON) * norm_gain).astype(jnp.bfloat16)
    logits = jnp.dot(normed.reshape(-1, width), router_weight, preferred_element_type=jnp.float32)
    picks = expert_ids.reshape(-1, 2)
    chosen = jnp.take_along_axis(logits, picks, axis=1)
    keep = keep_mask.reshape(-1, 2)
    gate_weights = jax.nn.sigmoid(chosen - chosen[:, ::-1]) * keep.astype(jnp.float32)
    experts = router_weight.shape[1]
    slots_here = requests_here * SLOT
    block_picks = expert_ids.reshape(requests_here, rows_here * 2)
    onehot = (block_picks[:, :, None] == jnp.arange(experts)[None, None, :]).astype(jnp.int32)
    ranks = jnp.sum((jnp.cumsum(onehot, axis=1) - 1) * onehot, axis=-1)
    places = (block_picks * slots_here + jnp.arange(requests_here)[:, None] * SLOT + ranks).reshape(
        -1
    )
    sent_rows = (normed[:, :, None, :] * keep_mask[:, :, :, None].astype(jnp.bfloat16)).reshape(
        -1, width
    )
    buffer = jnp.zeros((experts * slots_here, width), jnp.bfloat16).at[places].set(sent_rows)
    holders = lax.axis_size("req") // experts
    pair = [(r, r ^ 1) for r in range(lax.axis_size("req"))]
    other_gate = lax.ppermute(expert_gate, "req", pair)
    other_up = lax.ppermute(expert_up, "req", pair)
    other_down = lax.ppermute(expert_down, "req", pair)
    both_gate = jnp.stack([expert_gate, other_gate])
    both_up = jnp.stack([expert_up, other_up])
    both_down = jnp.stack([expert_down, other_down])
    step = slots_here // holders
    outgoing = buffer.reshape(experts * holders, step, width)
    arrived = lax.all_to_all(outgoing, "req", split_axis=0, concat_axis=0, tiled=True)
    gathered = lax.all_gather(arrived, "head", axis=0, tiled=False)
    flat_rows = gathered.reshape(-1, width)
    gate_val = jnp.einsum("nd,sdf->snf", flat_rows, both_gate, preferred_element_type=jnp.float32)
    up_val = jnp.einsum("nd,sdf->snf", flat_rows, both_up, preferred_element_type=jnp.float32)
    hidden = (jax.nn.gelu(gate_val, approximate=True) * up_val).astype(jnp.bfloat16)
    blocks_out = jnp.einsum(
        "snf,sfd->snd", hidden, both_down, preferred_element_type=jnp.float32
    ).astype(jnp.bfloat16)
    pair_sum = jnp.sum(blocks_out.astype(jnp.float32), axis=0).astype(jnp.bfloat16)
    shard_parts = lax.all_to_all(
        pair_sum.reshape(gathered.shape), "head", split_axis=0, concat_axis=0, tiled=True
    )
    full_sum = jnp.sum(shard_parts.astype(jnp.float32), axis=0).astype(jnp.bfloat16)
    returned = lax.all_to_all(full_sum, "req", split_axis=0, concat_axis=0, tiled=True)
    combined = returned.astype(jnp.float32).reshape(experts * slots_here, width)
    picked = jnp.take(combined, places, axis=0).reshape(-1, 2, width)
    mixture = jnp.sum(picked * gate_weights[:, :, None], axis=1)
    y_out = (
        (resid.reshape(-1, width) + mixture)
        .astype(jnp.bfloat16)
        .reshape(requests_here, rows_here, width)
    )
    return (y_out, new_keys, new_values)


def solution(mesh):
    return jax.shard_map(
        layer,
        mesh=mesh,
        in_specs=(
            P("req", ("head", "blk"), None),
            P("req", None, ("head", "blk")),
            P("req", None, ("head", "blk")),
            P("req", None, ("head", "blk")),
            P("req", None, ("head", "blk")),
            P("req", None, ("head", "blk")),
            P(None, None, ("head", "blk")),
            P(None, None, ("head", "blk")),
            P("req"),
            P("req"),
            P(("head", "blk"), None),
            P(),
            P(),
            P(None, ("req", "head")),
            P(None, ("req", "head")),
            P(("req", "head"), None),
            P("req", ("head", "blk"), None),
            P("req", ("head", "blk"), None),
        ),
        out_specs=(
            P("req", ("head", "blk"), None),
            P("req", ("head", "blk"), None),
            P("req", ("head", "blk"), None),
        ),
        check_vma=False,
    )
```

```python
import jax
import jax.numpy as jnp
from jax import lax
from jax.sharding import PartitionSpec as P

HD = 64
SLOT = 16


EPSILON = 1e-06


def attend_request(operands):
    (
        queries,
        keys_stretch,
        values_stretch,
        keys_cache,
        values_cache,
        keys_prefix,
        values_prefix,
        length,
    ) = operands
    heads_here = queries.shape[1] // HD
    prefix_rows = keys_prefix.shape[0]
    history_rows = keys_cache.shape[0]
    stretch_rows = queries.shape[0]
    keys_all = jnp.concatenate([keys_prefix, keys_cache, keys_stretch], 0).reshape(
        -1, heads_here, HD
    )
    values_all = jnp.concatenate([values_prefix, values_cache, values_stretch], 0).reshape(
        -1, heads_here, HD
    )
    key_pos = jnp.arange(keys_all.shape[0])
    query_pos = jnp.arange(stretch_rows)
    in_prefix = key_pos < prefix_rows
    in_history = (
        (key_pos >= prefix_rows)
        & (key_pos < prefix_rows + history_rows)
        & (key_pos - prefix_rows < length)
    )
    in_stretch = (key_pos[None, :] >= prefix_rows + history_rows) & (
        key_pos[None, :] - prefix_rows - history_rows <= query_pos[:, None]
    )
    visible = (in_prefix | in_history)[None, :] | in_stretch
    scores = jnp.einsum(
        "qhd,khd->hqk",
        queries.reshape(stretch_rows, heads_here, HD),
        keys_all,
        preferred_element_type=jnp.float32,
    ) * HD ** (-0.5)
    highest = jnp.max(jnp.where(visible[None], scores, -jnp.inf), axis=-1, keepdims=True)
    weights = jnp.where(visible[None], jnp.exp(scores - highest), 0.0)
    total = jnp.sum(weights, axis=-1, keepdims=True)
    rounded = weights.astype(jnp.bfloat16)
    mixed = jnp.einsum(
        "hqk,khd->qhd", rounded, values_all, preferred_element_type=jnp.float32
    ) / jnp.transpose(total, (1, 0, 2))
    return mixed.reshape(stretch_rows, -1).astype(jnp.bfloat16)


def extend(cache, stretch, length):
    hist = cache.shape[0]
    rows = stretch.shape[0]
    width = cache.shape[1]
    span = jnp.arange(hist + rows)
    padded_cache = jnp.concatenate([cache, jnp.zeros((rows, width), cache.dtype)], 0)
    framed = jnp.concatenate(
        [jnp.zeros((hist, width), stretch.dtype), stretch, jnp.zeros((hist, width), stretch.dtype)], 0
    )
    shifted = lax.dynamic_slice(framed, (hist - length, jnp.int32(0)), (hist + rows, width))
    return jnp.where((span < length)[:, None], padded_cache, shifted)


def to_positions(grown_keys, grown_values):
    groups = lax.axis_size(("head", "blk"))
    me = lax.axis_index(("head", "blk"))
    lead, rows, width = grown_keys.shape
    span = rows // groups
    parts = jnp.stack([grown_keys[0], grown_values[0]]).reshape(2, groups, span, width)
    blocks = [lax.dynamic_index_in_dim(parts, me, axis=1, keepdims=False)]
    for k in range(1, groups):
        block = lax.dynamic_index_in_dim(parts, (me + k) % groups, axis=1, keepdims=False)
        perm = [(i, (i + k) % groups) for i in range(groups)]
        blocks.append(lax.ppermute(block, ("head", "blk"), perm))
    stacked = jnp.stack(blocks, axis=1)
    order = (me - jnp.arange(groups)) % groups
    by_source = jnp.take(stacked, order, axis=1)
    joined = jnp.transpose(by_source, (0, 2, 1, 3)).reshape(2, lead, span, groups * width)
    return joined[0], joined[1]


def layer(
    x_tokens,
    query,
    key_new,
    value_new,
    cache_keys,
    cache_values,
    prefix_keys,
    prefix_values,
    history_len,
    group_ids,
    out_weight,
    norm_gain,
    router_weight,
    expert_gate,
    expert_up,
    expert_down,
    expert_ids,
    keep_mask,
):
    grown_keys = jax.vmap(extend)(cache_keys, key_new, history_len)
    grown_values = jax.vmap(extend)(cache_values, value_new, history_len)
    new_keys, new_values = to_positions(grown_keys, grown_values)
    chosen_keys = jnp.take(prefix_keys, group_ids, axis=0)
    chosen_values = jnp.take(prefix_values, group_ids, axis=0)
    attended = attend_request(
        (
            query[0],
            key_new[0],
            value_new[0],
            cache_keys[0],
            cache_values[0],
            chosen_keys[0],
            chosen_values[0],
            history_len[0],
        )
    )[None]
    requests_here = x_tokens.shape[0]
    rows_here = x_tokens.shape[1]
    width = x_tokens.shape[2]
    full_weight = lax.all_gather(out_weight, ("head", "blk"), axis=0, tiled=True)
    by_token = lax.all_to_all(attended, ("head", "blk"), split_axis=1, concat_axis=2, tiled=True)
    projected = jnp.einsum(
        "rqf,fd->rqd", by_token, full_weight, preferred_element_type=jnp.float32
    )
    resid = x_tokens.astype(jnp.float32) + projected
    mean_square = jnp.mean(resid * resid, axis=-1, keepdims=True)
    normed = (resid * lax.rsqrt(mean_square + EPSILON) * norm_gain).astype(jnp.bfloat16)
    logits = jnp.dot(normed.reshape(-1, width), router_weight, preferred_element_type=jnp.float32)
    picks = expert_ids.reshape(-1, 2)
    chosen = jnp.take_along_axis(logits, picks, axis=1)
    keep = keep_mask.reshape(-1, 2)
    gate_weights = jax.nn.sigmoid(chosen - chosen[:, ::-1]) * keep.astype(jnp.float32)
    experts = router_weight.shape[1]
    slots_here = requests_here * SLOT
    block_picks = expert_ids.reshape(requests_here, rows_here * 2)
    onehot = (block_picks[:, :, None] == jnp.arange(experts)[None, None, :]).astype(jnp.int32)
    ranks = jnp.sum((jnp.cumsum(onehot, axis=1) - 1) * onehot, axis=-1)
    places = (block_picks * slots_here + jnp.arange(requests_here)[:, None] * SLOT + ranks).reshape(
        -1
    )
    sent_rows = (normed[:, :, None, :] * keep_mask[:, :, :, None].astype(jnp.bfloat16)).reshape(
        -1, width
    )
    buffer = jnp.zeros((experts * slots_here, width), jnp.bfloat16).at[places].set(sent_rows)
    holders = lax.axis_size("req") // experts
    pair = [(r, r ^ 1) for r in range(lax.axis_size("req"))]
    other_gate = lax.ppermute(expert_gate, "req", pair)
    other_up = lax.ppermute(expert_up, "req", pair)
    other_down = lax.ppermute(expert_down, "req", pair)
    both_gate = jnp.stack([expert_gate, other_gate])
    both_up = jnp.stack([expert_up, other_up])
    both_down = jnp.stack([expert_down, other_down])
    step = slots_here // holders
    slabs = buffer.reshape(experts * holders, step, width)
    chunks = 2
    size = step // chunks
    pieces = []
    for c in range(chunks):
        outgoing = slabs[:, c * size:(c + 1) * size]
        arrived = lax.all_to_all(outgoing, "req", split_axis=0, concat_axis=0, tiled=True)
        gathered = lax.all_gather(arrived, "head", axis=0, tiled=False)
        flat_rows = gathered.reshape(-1, width)
        gate_val = jnp.einsum("nd,sdf->snf", flat_rows, both_gate, preferred_element_type=jnp.float32)
        up_val = jnp.einsum("nd,sdf->snf", flat_rows, both_up, preferred_element_type=jnp.float32)
        hidden = (jax.nn.gelu(gate_val, approximate=True) * up_val).astype(jnp.bfloat16)
        blocks_out = jnp.einsum(
            "snf,sfd->snd", hidden, both_down, preferred_element_type=jnp.float32
        ).astype(jnp.bfloat16)
        pair_sum = jnp.sum(blocks_out.astype(jnp.float32), axis=0).astype(jnp.bfloat16)
        shard_parts = lax.all_to_all(
            pair_sum.reshape(gathered.shape), "head", split_axis=0, concat_axis=0, tiled=True
        )
        full_sum = jnp.sum(shard_parts.astype(jnp.float32), axis=0).astype(jnp.bfloat16)
        pieces.append(lax.all_to_all(full_sum, "req", split_axis=0, concat_axis=0, tiled=True))
    returned = jnp.concatenate(pieces, axis=1)
    combined = returned.astype(jnp.float32).reshape(experts * slots_here, width)
    picked = jnp.take(combined, places, axis=0).reshape(-1, 2, width)
    mixture = jnp.sum(picked * gate_weights[:, :, None], axis=1)
    y_out = (
        (resid.reshape(-1, width) + mixture)
        .astype(jnp.bfloat16)
        .reshape(requests_here, rows_here, width)
    )
    return (y_out, new_keys, new_values)


def solution(mesh):
    return jax.shard_map(
        layer,
        mesh=mesh,
        in_specs=(
            P("req", ("head", "blk"), None),
            P("req", None, ("head", "blk")),
            P("req", None, ("head", "blk")),
            P("req", None, ("head", "blk")),
            P("req", None, ("head", "blk")),
            P("req", None, ("head", "blk")),
            P(None, None, ("head", "blk")),
            P(None, None, ("head", "blk")),
            P("req"),
            P("req"),
            P(("head", "blk"), None),
            P(),
            P(),
            P(None, ("req", "head")),
            P(None, ("req", "head")),
            P(("req", "head"), None),
            P("req", ("head", "blk"), None),
            P("req", ("head", "blk"), None),
        ),
        out_specs=(
            P("req", ("head", "blk"), None),
            P("req", ("head", "blk"), None),
            P("req", ("head", "blk"), None),
        ),
        check_vma=False,
    )
```

```python
import jax
import jax.numpy as jnp
from jax import lax
from jax.sharding import PartitionSpec as P

HD = 64
SLOT = 16


EPSILON = 1e-06


def attend_request(operands):
    (
        queries,
        keys_stretch,
        values_stretch,
        keys_cache,
        values_cache,
        keys_prefix,
        values_prefix,
        length,
    ) = operands
    heads_here = queries.shape[1] // HD
    prefix_rows = keys_prefix.shape[0]
    history_rows = keys_cache.shape[0]
    stretch_rows = queries.shape[0]
    keys_all = jnp.concatenate([keys_prefix, keys_cache, keys_stretch], 0).reshape(
        -1, heads_here, HD
    )
    values_all = jnp.concatenate([values_prefix, values_cache, values_stretch], 0).reshape(
        -1, heads_here, HD
    )
    key_pos = jnp.arange(keys_all.shape[0])
    query_pos = jnp.arange(stretch_rows)
    in_prefix = key_pos < prefix_rows
    in_history = (
        (key_pos >= prefix_rows)
        & (key_pos < prefix_rows + history_rows)
        & (key_pos - prefix_rows < length)
    )
    in_stretch = (key_pos[None, :] >= prefix_rows + history_rows) & (
        key_pos[None, :] - prefix_rows - history_rows <= query_pos[:, None]
    )
    visible = (in_prefix | in_history)[None, :] | in_stretch
    scores = jnp.einsum(
        "qhd,khd->hqk",
        queries.reshape(stretch_rows, heads_here, HD),
        keys_all,
        preferred_element_type=jnp.float32,
    ) * HD ** (-0.5)
    highest = jnp.max(jnp.where(visible[None], scores, -jnp.inf), axis=-1, keepdims=True)
    weights = jnp.where(visible[None], jnp.exp(scores - highest), 0.0)
    total = jnp.sum(weights, axis=-1, keepdims=True)
    rounded = weights.astype(jnp.bfloat16)
    mixed = jnp.einsum(
        "hqk,khd->qhd", rounded, values_all, preferred_element_type=jnp.float32
    ) / jnp.transpose(total, (1, 0, 2))
    return mixed.reshape(stretch_rows, -1).astype(jnp.bfloat16)


def extend(cache, stretch, length):
    hist = cache.shape[0]
    rows = stretch.shape[0]
    width = cache.shape[1]
    span = jnp.arange(hist + rows)
    padded_cache = jnp.concatenate([cache, jnp.zeros((rows, width), cache.dtype)], 0)
    framed = jnp.concatenate(
        [jnp.zeros((hist, width), stretch.dtype), stretch, jnp.zeros((hist, width), stretch.dtype)], 0
    )
    shifted = lax.dynamic_slice(framed, (hist - length, jnp.int32(0)), (hist + rows, width))
    return jnp.where((span < length)[:, None], padded_cache, shifted)


def to_positions(grown_keys, grown_values):
    groups = lax.axis_size(("head", "blk"))
    me = lax.axis_index(("head", "blk"))
    lead, rows, width = grown_keys.shape
    span = rows // groups
    parts = jnp.stack([grown_keys[0], grown_values[0]]).reshape(2, groups, span, width)
    blocks = [lax.dynamic_index_in_dim(parts, me, axis=1, keepdims=False)]
    for k in range(1, groups):
        block = lax.dynamic_index_in_dim(parts, (me + k) % groups, axis=1, keepdims=False)
        perm = [(i, (i + k) % groups) for i in range(groups)]
        blocks.append(lax.ppermute(block, ("head", "blk"), perm))
    stacked = jnp.stack(blocks, axis=1)
    order = (me - jnp.arange(groups)) % groups
    by_source = jnp.take(stacked, order, axis=1)
    joined = jnp.transpose(by_source, (0, 2, 1, 3)).reshape(2, lead, span, groups * width)
    return joined[0], joined[1]


def layer(
    x_tokens,
    query,
    key_new,
    value_new,
    cache_keys,
    cache_values,
    prefix_keys,
    prefix_values,
    history_len,
    group_ids,
    out_weight,
    norm_gain,
    router_weight,
    expert_gate,
    expert_up,
    expert_down,
    expert_ids,
    keep_mask,
):
    grown_keys = jax.vmap(extend)(cache_keys, key_new, history_len)
    grown_values = jax.vmap(extend)(cache_values, value_new, history_len)
    new_keys, new_values = to_positions(grown_keys, grown_values)
    chosen_keys = jnp.take(prefix_keys, group_ids, axis=0)
    chosen_values = jnp.take(prefix_values, group_ids, axis=0)
    groups = lax.axis_size(("head", "blk"))
    full_weight = lax.all_to_all(
        jnp.broadcast_to(out_weight[None], (groups,) + out_weight.shape),
        ("head", "blk"),
        split_axis=0,
        concat_axis=0,
        tiled=True,
    ).reshape(groups * out_weight.shape[0], out_weight.shape[1])
    full_weight, query = lax.optimization_barrier((full_weight, query))
    attended = attend_request(
        (
            query[0],
            key_new[0],
            value_new[0],
            cache_keys[0],
            cache_values[0],
            chosen_keys[0],
            chosen_values[0],
            history_len[0],
        )
    )[None]
    requests_here = x_tokens.shape[0]
    rows_here = x_tokens.shape[1]
    width = x_tokens.shape[2]
    by_token = lax.all_to_all(attended, ("head", "blk"), split_axis=1, concat_axis=2, tiled=True)
    projected = jnp.einsum(
        "rqf,fd->rqd", by_token, full_weight, preferred_element_type=jnp.float32
    )
    resid = x_tokens.astype(jnp.float32) + projected
    mean_square = jnp.mean(resid * resid, axis=-1, keepdims=True)
    normed = (resid * lax.rsqrt(mean_square + EPSILON) * norm_gain).astype(jnp.bfloat16)
    logits = jnp.dot(normed.reshape(-1, width), router_weight, preferred_element_type=jnp.float32)
    picks = expert_ids.reshape(-1, 2)
    chosen = jnp.take_along_axis(logits, picks, axis=1)
    keep = keep_mask.reshape(-1, 2)
    gate_weights = jax.nn.sigmoid(chosen - chosen[:, ::-1]) * keep.astype(jnp.float32)
    experts = router_weight.shape[1]
    slots_here = requests_here * SLOT
    block_picks = expert_ids.reshape(requests_here, rows_here * 2)
    onehot = (block_picks[:, :, None] == jnp.arange(experts)[None, None, :]).astype(jnp.int32)
    ranks = jnp.sum((jnp.cumsum(onehot, axis=1) - 1) * onehot, axis=-1)
    places = (block_picks * slots_here + jnp.arange(requests_here)[:, None] * SLOT + ranks).reshape(
        -1
    )
    sent_rows = (normed[:, :, None, :] * keep_mask[:, :, :, None].astype(jnp.bfloat16)).reshape(
        -1, width
    )
    buffer = jnp.zeros((experts * slots_here, width), jnp.bfloat16).at[places].set(sent_rows)
    holders = lax.axis_size("req") // experts
    pair = [(r, r ^ 1) for r in range(lax.axis_size("req"))]
    other_gate = lax.ppermute(expert_gate, "req", pair)
    other_up = lax.ppermute(expert_up, "req", pair)
    other_down = lax.ppermute(expert_down, "req", pair)
    both_gate = jnp.stack([expert_gate, other_gate])
    both_up = jnp.stack([expert_up, other_up])
    both_down = jnp.stack([expert_down, other_down])
    step = slots_here // holders
    outgoing = buffer.reshape(experts * holders, step, width)
    arrived = lax.all_to_all(outgoing, "req", split_axis=0, concat_axis=0, tiled=True)
    peers = lax.axis_size("head")
    gathered = lax.all_to_all(
        jnp.broadcast_to(arrived[None], (peers,) + arrived.shape),
        "head",
        split_axis=0,
        concat_axis=0,
        tiled=True,
    )
    flat_rows = gathered.reshape(-1, width)
    gate_val = jnp.einsum("nd,sdf->snf", flat_rows, both_gate, preferred_element_type=jnp.float32)
    up_val = jnp.einsum("nd,sdf->snf", flat_rows, both_up, preferred_element_type=jnp.float32)
    hidden = (jax.nn.gelu(gate_val, approximate=True) * up_val).astype(jnp.bfloat16)
    blocks_out = jnp.einsum(
        "snf,sfd->snd", hidden, both_down, preferred_element_type=jnp.float32
    ).astype(jnp.bfloat16)
    pair_sum = jnp.sum(blocks_out.astype(jnp.float32), axis=0).astype(jnp.bfloat16)
    shard_parts = lax.all_to_all(
        pair_sum.reshape(gathered.shape), "head", split_axis=0, concat_axis=0, tiled=True
    )
    full_sum = jnp.sum(shard_parts.astype(jnp.float32), axis=0).astype(jnp.bfloat16)
    returned = lax.all_to_all(full_sum, "req", split_axis=0, concat_axis=0, tiled=True)
    combined = returned.astype(jnp.float32).reshape(experts * slots_here, width)
    picked = jnp.take(combined, places, axis=0).reshape(-1, 2, width)
    mixture = jnp.sum(picked * gate_weights[:, :, None], axis=1)
    y_out = (
        (resid.reshape(-1, width) + mixture)
        .astype(jnp.bfloat16)
        .reshape(requests_here, rows_here, width)
    )
    return (y_out, new_keys, new_values)


def solution(mesh):
    return jax.shard_map(
        layer,
        mesh=mesh,
        in_specs=(
            P("req", ("head", "blk"), None),
            P("req", None, ("head", "blk")),
            P("req", None, ("head", "blk")),
            P("req", None, ("head", "blk")),
            P("req", None, ("head", "blk")),
            P("req", None, ("head", "blk")),
            P(None, None, ("head", "blk")),
            P(None, None, ("head", "blk")),
            P("req"),
            P("req"),
            P(("head", "blk"), None),
            P(),
            P(),
            P(None, ("req", "head")),
            P(None, ("req", "head")),
            P(("req", "head"), None),
            P("req", ("head", "blk"), None),
            P("req", ("head", "blk"), None),
        ),
        out_specs=(
            P("req", ("head", "blk"), None),
            P("req", ("head", "blk"), None),
            P("req", ("head", "blk"), None),
        ),
        check_vma=False,
    )
```

```python
import jax
import jax.numpy as jnp
from jax import lax
from jax.sharding import PartitionSpec as P

HD = 64
SLOT = 16


EPSILON = 1e-06


def attend_request(operands):
    (
        queries,
        keys_stretch,
        values_stretch,
        keys_cache,
        values_cache,
        keys_prefix,
        values_prefix,
        length,
    ) = operands
    heads_here = queries.shape[1] // HD
    prefix_rows = keys_prefix.shape[0]
    history_rows = keys_cache.shape[0]
    stretch_rows = queries.shape[0]
    keys_all = jnp.concatenate([keys_prefix, keys_cache, keys_stretch], 0).reshape(
        -1, heads_here, HD
    )
    values_all = jnp.concatenate([values_prefix, values_cache, values_stretch], 0).reshape(
        -1, heads_here, HD
    )
    key_pos = jnp.arange(keys_all.shape[0])
    query_pos = jnp.arange(stretch_rows)
    in_prefix = key_pos < prefix_rows
    in_history = (
        (key_pos >= prefix_rows)
        & (key_pos < prefix_rows + history_rows)
        & (key_pos - prefix_rows < length)
    )
    in_stretch = (key_pos[None, :] >= prefix_rows + history_rows) & (
        key_pos[None, :] - prefix_rows - history_rows <= query_pos[:, None]
    )
    visible = (in_prefix | in_history)[None, :] | in_stretch
    scores = jnp.einsum(
        "qhd,khd->hqk",
        queries.reshape(stretch_rows, heads_here, HD),
        keys_all,
        preferred_element_type=jnp.float32,
    ) * HD ** (-0.5)
    highest = jnp.max(jnp.where(visible[None], scores, -jnp.inf), axis=-1, keepdims=True)
    weights = jnp.where(visible[None], jnp.exp(scores - highest), 0.0)
    total = jnp.sum(weights, axis=-1, keepdims=True)
    rounded = weights.astype(jnp.bfloat16)
    mixed = jnp.einsum(
        "hqk,khd->qhd", rounded, values_all, preferred_element_type=jnp.float32
    ) / jnp.transpose(total, (1, 0, 2))
    return mixed.reshape(stretch_rows, -1).astype(jnp.bfloat16)


def extend(cache, stretch, length):
    hist = cache.shape[0]
    rows = stretch.shape[0]
    width = cache.shape[1]
    span = jnp.arange(hist + rows)
    padded_cache = jnp.concatenate([cache, jnp.zeros((rows, width), cache.dtype)], 0)
    framed = jnp.concatenate(
        [jnp.zeros((hist, width), stretch.dtype), stretch, jnp.zeros((hist, width), stretch.dtype)], 0
    )
    shifted = lax.dynamic_slice(framed, (hist - length, jnp.int32(0)), (hist + rows, width))
    return jnp.where((span < length)[:, None], padded_cache, shifted)


def to_positions(grown_keys, grown_values):
    groups = lax.axis_size(("head", "blk"))
    lead, rows, width = grown_keys.shape
    parts = jnp.stack([grown_keys, grown_values]).reshape(2 * lead, groups, rows // groups, width)
    got = lax.all_to_all(parts, ("head", "blk"), split_axis=1, concat_axis=1, tiled=True)
    joined = jnp.transpose(got, (0, 2, 1, 3)).reshape(2, lead, rows // groups, groups * width)
    return joined[0], joined[1]


def layer(
    x_tokens,
    query,
    key_new,
    value_new,
    cache_keys,
    cache_values,
    prefix_keys,
    prefix_values,
    history_len,
    group_ids,
    out_weight,
    norm_gain,
    router_weight,
    expert_gate,
    expert_up,
    expert_down,
    expert_ids,
    keep_mask,
):
    grown_keys = jax.vmap(extend)(cache_keys, key_new, history_len)
    grown_values = jax.vmap(extend)(cache_values, value_new, history_len)
    new_keys, new_values = to_positions(grown_keys, grown_values)
    new_keys, new_values, query = lax.optimization_barrier((new_keys, new_values, query))
    chosen_keys = jnp.take(prefix_keys, group_ids, axis=0)
    chosen_values = jnp.take(prefix_values, group_ids, axis=0)
    attended = attend_request(
        (
            query[0],
            key_new[0],
            value_new[0],
            cache_keys[0],
            cache_values[0],
            chosen_keys[0],
            chosen_values[0],
            history_len[0],
        )
    )[None]
    requests_here = x_tokens.shape[0]
    rows_here = x_tokens.shape[1]
    width = x_tokens.shape[2]
    full_weight = lax.all_gather(out_weight, ("head", "blk"), axis=0, tiled=True)
    by_token = lax.all_to_all(attended, ("head", "blk"), split_axis=1, concat_axis=2, tiled=True)
    projected = jnp.einsum(
        "rqf,fd->rqd", by_token, full_weight, preferred_element_type=jnp.float32
    )
    resid = x_tokens.astype(jnp.float32) + projected
    mean_square = jnp.mean(resid * resid, axis=-1, keepdims=True)
    normed = (resid * lax.rsqrt(mean_square + EPSILON) * norm_gain).astype(jnp.bfloat16)
    logits = jnp.dot(normed.reshape(-1, width), router_weight, preferred_element_type=jnp.float32)
    picks = expert_ids.reshape(-1, 2)
    chosen = jnp.take_along_axis(logits, picks, axis=1)
    keep = keep_mask.reshape(-1, 2)
    gate_weights = jax.nn.sigmoid(chosen - chosen[:, ::-1]) * keep.astype(jnp.float32)
    experts = router_weight.shape[1]
    slots_here = requests_here * SLOT
    block_picks = expert_ids.reshape(requests_here, rows_here * 2)
    onehot = (block_picks[:, :, None] == jnp.arange(experts)[None, None, :]).astype(jnp.int32)
    ranks = jnp.sum((jnp.cumsum(onehot, axis=1) - 1) * onehot, axis=-1)
    places = (block_picks * slots_here + jnp.arange(requests_here)[:, None] * SLOT + ranks).reshape(
        -1
    )
    sent_rows = (normed[:, :, None, :] * keep_mask[:, :, :, None].astype(jnp.bfloat16)).reshape(
        -1, width
    )
    buffer = jnp.zeros((experts * slots_here, width), jnp.bfloat16).at[places].set(sent_rows)
    holders = lax.axis_size("req") // experts
    pair = [(r, r ^ 1) for r in range(lax.axis_size("req"))]
    other_gate = lax.ppermute(expert_gate, "req", pair)
    other_up = lax.ppermute(expert_up, "req", pair)
    other_down = lax.ppermute(expert_down, "req", pair)
    both_gate = jnp.stack([expert_gate, other_gate])
    both_up = jnp.stack([expert_up, other_up])
    both_down = jnp.stack([expert_down, other_down])
    step = slots_here // holders
    outgoing = buffer.reshape(experts * holders, step, width)
    arrived = lax.all_to_all(outgoing, "req", split_axis=0, concat_axis=0, tiled=True)
    gathered = lax.all_gather(arrived, "head", axis=0, tiled=False)
    flat_rows = gathered.reshape(-1, width)
    gate_val = jnp.einsum("nd,sdf->snf", flat_rows, both_gate, preferred_element_type=jnp.float32)
    up_val = jnp.einsum("nd,sdf->snf", flat_rows, both_up, preferred_element_type=jnp.float32)
    hidden = (jax.nn.gelu(gate_val, approximate=True) * up_val).astype(jnp.bfloat16)
    blocks_out = jnp.einsum(
        "snf,sfd->snd", hidden, both_down, preferred_element_type=jnp.float32
    ).astype(jnp.bfloat16)
    pair_sum = jnp.sum(blocks_out.astype(jnp.float32), axis=0).astype(jnp.bfloat16)
    shard_parts = lax.all_to_all(
        pair_sum.reshape(gathered.shape), "head", split_axis=0, concat_axis=0, tiled=True
    )
    full_sum = jnp.sum(shard_parts.astype(jnp.float32), axis=0).astype(jnp.bfloat16)
    returned = lax.all_to_all(full_sum, "req", split_axis=0, concat_axis=0, tiled=True)
    combined = returned.astype(jnp.float32).reshape(experts * slots_here, width)
    picked = jnp.take(combined, places, axis=0).reshape(-1, 2, width)
    mixture = jnp.sum(picked * gate_weights[:, :, None], axis=1)
    y_out = (
        (resid.reshape(-1, width) + mixture)
        .astype(jnp.bfloat16)
        .reshape(requests_here, rows_here, width)
    )
    return (y_out, new_keys, new_values)


def solution(mesh):
    return jax.shard_map(
        layer,
        mesh=mesh,
        in_specs=(
            P("req", ("head", "blk"), None),
            P("req", None, ("head", "blk")),
            P("req", None, ("head", "blk")),
            P("req", None, ("head", "blk")),
            P("req", None, ("head", "blk")),
            P("req", None, ("head", "blk")),
            P(None, None, ("head", "blk")),
            P(None, None, ("head", "blk")),
            P("req"),
            P("req"),
            P(("head", "blk"), None),
            P(),
            P(),
            P(None, ("req", "head")),
            P(None, ("req", "head")),
            P(("req", "head"), None),
            P("req", ("head", "blk"), None),
            P("req", ("head", "blk"), None),
        ),
        out_specs=(
            P("req", ("head", "blk"), None),
            P("req", ("head", "blk"), None),
            P("req", ("head", "blk"), None),
        ),
        check_vma=False,
    )
```

```python
import jax
import jax.numpy as jnp
from jax import lax
from jax.sharding import PartitionSpec as P

HD = 64
SLOT = 16


EPSILON = 1e-06


def attend_request(operands):
    (
        queries,
        keys_stretch,
        values_stretch,
        keys_cache,
        values_cache,
        keys_prefix,
        values_prefix,
        length,
    ) = operands
    heads_here = queries.shape[1] // HD
    prefix_rows = keys_prefix.shape[0]
    history_rows = keys_cache.shape[0]
    stretch_rows = queries.shape[0]
    keys_all = jnp.concatenate([keys_prefix, keys_cache, keys_stretch], 0).reshape(
        -1, heads_here, HD
    )
    values_all = jnp.concatenate([values_prefix, values_cache, values_stretch], 0).reshape(
        -1, heads_here, HD
    )
    key_pos = jnp.arange(keys_all.shape[0])
    query_pos = jnp.arange(stretch_rows)
    in_prefix = key_pos < prefix_rows
    in_history = (
        (key_pos >= prefix_rows)
        & (key_pos < prefix_rows + history_rows)
        & (key_pos - prefix_rows < length)
    )
    in_stretch = (key_pos[None, :] >= prefix_rows + history_rows) & (
        key_pos[None, :] - prefix_rows - history_rows <= query_pos[:, None]
    )
    visible = (in_prefix | in_history)[None, :] | in_stretch
    scores = jnp.einsum(
        "qhd,khd->hqk",
        queries.reshape(stretch_rows, heads_here, HD),
        keys_all,
        preferred_element_type=jnp.float32,
    ) * HD ** (-0.5)
    highest = jnp.max(jnp.where(visible[None], scores, -jnp.inf), axis=-1, keepdims=True)
    weights = jnp.where(visible[None], jnp.exp(scores - highest), 0.0)
    total = jnp.sum(weights, axis=-1, keepdims=True)
    rounded = weights.astype(jnp.bfloat16)
    mixed = jnp.einsum(
        "hqk,khd->qhd", rounded, values_all, preferred_element_type=jnp.float32
    ) / jnp.transpose(total, (1, 0, 2))
    return mixed.reshape(stretch_rows, -1).astype(jnp.bfloat16)


def extend(cache, stretch, length):
    hist = cache.shape[0]
    rows = stretch.shape[0]
    width = cache.shape[1]
    span = jnp.arange(hist + rows)
    padded_cache = jnp.concatenate([cache, jnp.zeros((rows, width), cache.dtype)], 0)
    framed = jnp.concatenate(
        [jnp.zeros((hist, width), stretch.dtype), stretch, jnp.zeros((hist, width), stretch.dtype)], 0
    )
    shifted = lax.dynamic_slice(framed, (hist - length, jnp.int32(0)), (hist + rows, width))
    return jnp.where((span < length)[:, None], padded_cache, shifted)


def to_positions(grown_keys, grown_values):
    heads = lax.axis_size("head")
    cores = lax.axis_size("blk")
    me_h = lax.axis_index("head")
    me_b = lax.axis_index("blk")
    lead, rows, width = grown_keys.shape
    span = rows // (heads * cores)
    parts = jnp.stack([grown_keys[0], grown_values[0]]).reshape(2, heads, cores, span, width)
    keep = lax.dynamic_index_in_dim(parts, me_b, axis=2, keepdims=False)
    sent = lax.dynamic_index_in_dim(parts, 1 - me_b, axis=2, keepdims=False)
    got = lax.ppermute(sent, "blk", [(0, 1), (1, 0)])
    first = jnp.where(me_b == 0, keep, got)
    second = jnp.where(me_b == 0, got, keep)
    mine = jnp.concatenate([first, second], axis=-1)
    blocks = [lax.dynamic_index_in_dim(mine, me_h, axis=1, keepdims=False)]
    for k in range(1, heads):
        block = lax.dynamic_index_in_dim(mine, (me_h + k) % heads, axis=1, keepdims=False)
        perm = [(i, (i + k) % heads) for i in range(heads)]
        blocks.append(lax.ppermute(block, "head", perm))
    stacked = jnp.stack(blocks, axis=1)
    order = (me_h - jnp.arange(heads)) % heads
    by_source = jnp.take(stacked, order, axis=1)
    joined = jnp.transpose(by_source, (0, 2, 1, 3)).reshape(2, lead, span, heads * cores * width)
    return joined[0], joined[1]


def layer(
    x_tokens,
    query,
    key_new,
    value_new,
    cache_keys,
    cache_values,
    prefix_keys,
    prefix_values,
    history_len,
    group_ids,
    out_weight,
    norm_gain,
    router_weight,
    expert_gate,
    expert_up,
    expert_down,
    expert_ids,
    keep_mask,
):
    grown_keys = jax.vmap(extend)(cache_keys, key_new, history_len)
    grown_values = jax.vmap(extend)(cache_values, value_new, history_len)
    new_keys, new_values = to_positions(grown_keys, grown_values)
    chosen_keys = jnp.take(prefix_keys, group_ids, axis=0)
    chosen_values = jnp.take(prefix_values, group_ids, axis=0)
    attended = attend_request(
        (
            query[0],
            key_new[0],
            value_new[0],
            cache_keys[0],
            cache_values[0],
            chosen_keys[0],
            chosen_values[0],
            history_len[0],
        )
    )[None]
    requests_here = x_tokens.shape[0]
    rows_here = x_tokens.shape[1]
    width = x_tokens.shape[2]
    full_weight = lax.all_gather(out_weight, ("head", "blk"), axis=0, tiled=True)
    by_token = lax.all_to_all(attended, ("head", "blk"), split_axis=1, concat_axis=2, tiled=True)
    projected = jnp.einsum(
        "rqf,fd->rqd", by_token, full_weight, preferred_element_type=jnp.float32
    )
    resid = x_tokens.astype(jnp.float32) + projected
    mean_square = jnp.mean(resid * resid, axis=-1, keepdims=True)
    normed = (resid * lax.rsqrt(mean_square + EPSILON) * norm_gain).astype(jnp.bfloat16)
    logits = jnp.dot(normed.reshape(-1, width), router_weight, preferred_element_type=jnp.float32)
    picks = expert_ids.reshape(-1, 2)
    chosen = jnp.take_along_axis(logits, picks, axis=1)
    keep = keep_mask.reshape(-1, 2)
    gate_weights = jax.nn.sigmoid(chosen - chosen[:, ::-1]) * keep.astype(jnp.float32)
    experts = router_weight.shape[1]
    slots_here = requests_here * SLOT
    block_picks = expert_ids.reshape(requests_here, rows_here * 2)
    onehot = (block_picks[:, :, None] == jnp.arange(experts)[None, None, :]).astype(jnp.int32)
    ranks = jnp.sum((jnp.cumsum(onehot, axis=1) - 1) * onehot, axis=-1)
    places = (block_picks * slots_here + jnp.arange(requests_here)[:, None] * SLOT + ranks).reshape(
        -1
    )
    sent_rows = (normed[:, :, None, :] * keep_mask[:, :, :, None].astype(jnp.bfloat16)).reshape(
        -1, width
    )
    buffer = jnp.zeros((experts * slots_here, width), jnp.bfloat16).at[places].set(sent_rows)
    holders = lax.axis_size("req") // experts
    pair = [(r, r ^ 1) for r in range(lax.axis_size("req"))]
    other_gate = lax.ppermute(expert_gate, "req", pair)
    other_up = lax.ppermute(expert_up, "req", pair)
    other_down = lax.ppermute(expert_down, "req", pair)
    both_gate = jnp.stack([expert_gate, other_gate])
    both_up = jnp.stack([expert_up, other_up])
    both_down = jnp.stack([expert_down, other_down])
    step = slots_here // holders
    outgoing = buffer.reshape(experts * holders, step, width)
    arrived = lax.all_to_all(outgoing, "req", split_axis=0, concat_axis=0, tiled=True)
    gathered = lax.all_gather(arrived, "head", axis=0, tiled=False)
    flat_rows = gathered.reshape(-1, width)
    gate_val = jnp.einsum("nd,sdf->snf", flat_rows, both_gate, preferred_element_type=jnp.float32)
    up_val = jnp.einsum("nd,sdf->snf", flat_rows, both_up, preferred_element_type=jnp.float32)
    hidden = (jax.nn.gelu(gate_val, approximate=True) * up_val).astype(jnp.bfloat16)
    blocks_out = jnp.einsum(
        "snf,sfd->snd", hidden, both_down, preferred_element_type=jnp.float32
    ).astype(jnp.bfloat16)
    pair_sum = jnp.sum(blocks_out.astype(jnp.float32), axis=0).astype(jnp.bfloat16)
    shard_parts = lax.all_to_all(
        pair_sum.reshape(gathered.shape), "head", split_axis=0, concat_axis=0, tiled=True
    )
    full_sum = jnp.sum(shard_parts.astype(jnp.float32), axis=0).astype(jnp.bfloat16)
    returned = lax.all_to_all(full_sum, "req", split_axis=0, concat_axis=0, tiled=True)
    combined = returned.astype(jnp.float32).reshape(experts * slots_here, width)
    picked = jnp.take(combined, places, axis=0).reshape(-1, 2, width)
    mixture = jnp.sum(picked * gate_weights[:, :, None], axis=1)
    y_out = (
        (resid.reshape(-1, width) + mixture)
        .astype(jnp.bfloat16)
        .reshape(requests_here, rows_here, width)
    )
    return (y_out, new_keys, new_values)


def solution(mesh):
    return jax.shard_map(
        layer,
        mesh=mesh,
        in_specs=(
            P("req", ("head", "blk"), None),
            P("req", None, ("head", "blk")),
            P("req", None, ("head", "blk")),
            P("req", None, ("head", "blk")),
            P("req", None, ("head", "blk")),
            P("req", None, ("head", "blk")),
            P(None, None, ("head", "blk")),
            P(None, None, ("head", "blk")),
            P("req"),
            P("req"),
            P(("head", "blk"), None),
            P(),
            P(),
            P(None, ("req", "head")),
            P(None, ("req", "head")),
            P(("req", "head"), None),
            P("req", ("head", "blk"), None),
            P("req", ("head", "blk"), None),
        ),
        out_specs=(
            P("req", ("head", "blk"), None),
            P("req", ("head", "blk"), None),
            P("req", ("head", "blk"), None),
        ),
        check_vma=False,
    )
```

```python
import jax
import jax.numpy as jnp
from jax import lax
from jax.sharding import PartitionSpec as P

HD = 64
SLOT = 16


EPSILON = 1e-06


def attend_request(operands):
    (
        queries,
        keys_stretch,
        values_stretch,
        keys_cache,
        values_cache,
        keys_prefix,
        values_prefix,
        length,
    ) = operands
    heads_here = queries.shape[1] // HD
    prefix_rows = keys_prefix.shape[0]
    history_rows = keys_cache.shape[0]
    stretch_rows = queries.shape[0]
    keys_all = jnp.concatenate([keys_prefix, keys_cache, keys_stretch], 0).reshape(
        -1, heads_here, HD
    )
    values_all = jnp.concatenate([values_prefix, values_cache, values_stretch], 0).reshape(
        -1, heads_here, HD
    )
    key_pos = jnp.arange(keys_all.shape[0])
    query_pos = jnp.arange(stretch_rows)
    in_prefix = key_pos < prefix_rows
    in_history = (
        (key_pos >= prefix_rows)
        & (key_pos < prefix_rows + history_rows)
        & (key_pos - prefix_rows < length)
    )
    in_stretch = (key_pos[None, :] >= prefix_rows + history_rows) & (
        key_pos[None, :] - prefix_rows - history_rows <= query_pos[:, None]
    )
    visible = (in_prefix | in_history)[None, :] | in_stretch
    scores = jnp.einsum(
        "qhd,khd->hqk",
        queries.reshape(stretch_rows, heads_here, HD),
        keys_all,
        preferred_element_type=jnp.float32,
    ) * HD ** (-0.5)
    highest = jnp.max(jnp.where(visible[None], scores, -jnp.inf), axis=-1, keepdims=True)
    weights = jnp.where(visible[None], jnp.exp(scores - highest), 0.0)
    total = jnp.sum(weights, axis=-1, keepdims=True)
    rounded = weights.astype(jnp.bfloat16)
    mixed = jnp.einsum(
        "hqk,khd->qhd", rounded, values_all, preferred_element_type=jnp.float32
    ) / jnp.transpose(total, (1, 0, 2))
    return mixed.reshape(stretch_rows, -1).astype(jnp.bfloat16)


def extend(cache, stretch, length):
    hist = cache.shape[0]
    rows = stretch.shape[0]
    width = cache.shape[1]
    span = jnp.arange(hist + rows)
    padded_cache = jnp.concatenate([cache, jnp.zeros((rows, width), cache.dtype)], 0)
    framed = jnp.concatenate(
        [jnp.zeros((hist, width), stretch.dtype), stretch, jnp.zeros((hist, width), stretch.dtype)], 0
    )
    shifted = lax.dynamic_slice(framed, (hist - length, jnp.int32(0)), (hist + rows, width))
    return jnp.where((span < length)[:, None], padded_cache, shifted)


def to_positions(grown_keys, grown_values):
    groups = lax.axis_size(("head", "blk"))
    me = lax.axis_index(("head", "blk"))
    lead, rows, width = grown_keys.shape
    span = rows // groups
    parts = jnp.stack([grown_keys[0], grown_values[0]]).reshape(2, groups, span, width)
    blocks = [lax.dynamic_index_in_dim(parts, me, axis=1, keepdims=False)]
    for k in range(1, groups):
        block = lax.dynamic_index_in_dim(parts, (me + k) % groups, axis=1, keepdims=False)
        perm = [(i, (i + k) % groups) for i in range(groups)]
        blocks.append(lax.ppermute(block, ("head", "blk"), perm))
    stacked = jnp.stack(blocks, axis=1)
    order = (me - jnp.arange(groups)) % groups
    by_source = jnp.take(stacked, order, axis=1)
    joined = jnp.transpose(by_source, (0, 2, 1, 3)).reshape(2, lead, span, groups * width)
    return joined[0], joined[1]


def layer(
    x_tokens,
    query,
    key_new,
    value_new,
    cache_keys,
    cache_values,
    prefix_keys,
    prefix_values,
    history_len,
    group_ids,
    out_weight,
    norm_gain,
    router_weight,
    expert_gate,
    expert_up,
    expert_down,
    expert_ids,
    keep_mask,
):
    grown_keys = jax.vmap(extend)(cache_keys, key_new, history_len)
    grown_values = jax.vmap(extend)(cache_values, value_new, history_len)
    new_keys, new_values = to_positions(grown_keys, grown_values)
    chosen_keys = jnp.take(prefix_keys, group_ids, axis=0)
    chosen_values = jnp.take(prefix_values, group_ids, axis=0)
    attended = attend_request(
        (
            query[0],
            key_new[0],
            value_new[0],
            cache_keys[0],
            cache_values[0],
            chosen_keys[0],
            chosen_values[0],
            history_len[0],
        )
    )[None]
    requests_here = x_tokens.shape[0]
    rows_here = x_tokens.shape[1]
    width = x_tokens.shape[2]
    full_weight = lax.all_gather(out_weight, ("head", "blk"), axis=0, tiled=True)
    by_token = lax.all_to_all(attended, ("head", "blk"), split_axis=1, concat_axis=2, tiled=True)
    projected = jnp.einsum(
        "rqf,fd->rqd", by_token, full_weight, preferred_element_type=jnp.float32
    )
    resid = x_tokens.astype(jnp.float32) + projected
    mean_square = jnp.mean(resid * resid, axis=-1, keepdims=True)
    normed = (resid * lax.rsqrt(mean_square + EPSILON) * norm_gain).astype(jnp.bfloat16)
    logits = jnp.dot(normed.reshape(-1, width), router_weight, preferred_element_type=jnp.float32)
    picks = expert_ids.reshape(-1, 2)
    chosen = jnp.take_along_axis(logits, picks, axis=1)
    keep = keep_mask.reshape(-1, 2)
    gate_weights = jax.nn.sigmoid(chosen - chosen[:, ::-1]) * keep.astype(jnp.float32)
    experts = router_weight.shape[1]
    slots_here = requests_here * SLOT
    block_picks = expert_ids.reshape(requests_here, rows_here * 2)
    onehot = (block_picks[:, :, None] == jnp.arange(experts)[None, None, :]).astype(jnp.int32)
    ranks = jnp.sum((jnp.cumsum(onehot, axis=1) - 1) * onehot, axis=-1)
    places = (block_picks * slots_here + jnp.arange(requests_here)[:, None] * SLOT + ranks).reshape(
        -1
    )
    sent_rows = (normed[:, :, None, :] * keep_mask[:, :, :, None].astype(jnp.bfloat16)).reshape(
        -1, width
    )
    buffer = jnp.zeros((experts * slots_here, width), jnp.bfloat16).at[places].set(sent_rows)
    holders = lax.axis_size("req") // experts
    pair = [(r, r ^ 1) for r in range(lax.axis_size("req"))]
    other_gate = lax.ppermute(expert_gate, "req", pair)
    other_up = lax.ppermute(expert_up, "req", pair)
    other_down = lax.ppermute(expert_down, "req", pair)
    step = slots_here // holders
    outgoing = buffer.reshape(experts * holders, step, width)
    arrived = lax.all_to_all(outgoing, "req", split_axis=0, concat_axis=0, tiled=True)
    gathered = lax.all_gather(arrived, "head", axis=0, tiled=False)
    flat_rows = gathered.reshape(-1, width)

    def serve(w_gate, w_up, w_down):
        gate_val = jnp.dot(flat_rows, w_gate, preferred_element_type=jnp.float32)
        up_val = jnp.dot(flat_rows, w_up, preferred_element_type=jnp.float32)
        hidden = (jax.nn.gelu(gate_val, approximate=True) * up_val).astype(jnp.bfloat16)
        return jnp.dot(hidden, w_down, preferred_element_type=jnp.float32).astype(jnp.bfloat16)

    own_out = serve(expert_gate, expert_up, expert_down)
    other_out = serve(other_gate, other_up, other_down)
    pair_sum = (own_out.astype(jnp.float32) + other_out.astype(jnp.float32)).astype(jnp.bfloat16)
    shard_parts = lax.all_to_all(
        pair_sum.reshape(gathered.shape), "head", split_axis=0, concat_axis=0, tiled=True
    )
    full_sum = jnp.sum(shard_parts.astype(jnp.float32), axis=0).astype(jnp.bfloat16)
    returned = lax.all_to_all(full_sum, "req", split_axis=0, concat_axis=0, tiled=True)
    combined = returned.astype(jnp.float32).reshape(experts * slots_here, width)
    picked = jnp.take(combined, places, axis=0).reshape(-1, 2, width)
    mixture = jnp.sum(picked * gate_weights[:, :, None], axis=1)
    y_out = (
        (resid.reshape(-1, width) + mixture)
        .astype(jnp.bfloat16)
        .reshape(requests_here, rows_here, width)
    )
    return (y_out, new_keys, new_values)


def solution(mesh):
    return jax.shard_map(
        layer,
        mesh=mesh,
        in_specs=(
            P("req", ("head", "blk"), None),
            P("req", None, ("head", "blk")),
            P("req", None, ("head", "blk")),
            P("req", None, ("head", "blk")),
            P("req", None, ("head", "blk")),
            P("req", None, ("head", "blk")),
            P(None, None, ("head", "blk")),
            P(None, None, ("head", "blk")),
            P("req"),
            P("req"),
            P(("head", "blk"), None),
            P(),
            P(),
            P(None, ("req", "head")),
            P(None, ("req", "head")),
            P(("req", "head"), None),
            P("req", ("head", "blk"), None),
            P("req", ("head", "blk"), None),
        ),
        out_specs=(
            P("req", ("head", "blk"), None),
            P("req", ("head", "blk"), None),
            P("req", ("head", "blk"), None),
        ),
        check_vma=False,
    )
```
